32 devices in a mesh: atoms: 8 (over y, x, core), bands: 4 (over z).
Axes of the slice: x: 2, y: 2, z: 4, core: 2. Of those that a mesh axis runs over, the one named last changes fastest.
Arguments:
- subspace: bfloat16 [512, 6144], P('bands', 'atoms'), may hold values from -120 to 120
- diag_block: bfloat16 [6144, 768], P('atoms'), may hold values from -0.0625 to 0.0625
- pair_block: bfloat16 [2, 6144, 768], P(None, 'atoms'), may hold values from -0.0625 to 0.0625
- pair_pattern: int32 [2, 32, 4], P(None, 'atoms'), may hold values 0 or 1
- atom_sizes: int32 [8, 4], replicated, may hold values from 1 to 256, 768 in all within a row
- rotations: bfloat16 [4, 512, 512], P(None, None, 'bands'), may hold values from -0.25 to 0.25
Outputs:
- rotated: float32 [512, 6144], P('bands', 'atoms')
The draws below stay inside these ranges and needn't reach their ends.
Inputs may be any that keep to these rules, and one draw needn't show every extreme that they name: `atom_sizes`: each row holds the orbital counts of the 4 atoms of one partition in order and sums to 768.
All inputs are finite; a program needn't handle non-finite values. No bound on the sum of `pair_pattern` on one device may be relied on, other than what follows from the above.
Results may differ from the reference program's by a relative error of at most 0.028.
Values may be sent and summed in bfloat16 or wider, within the bound.
No kernel may reach another device: no remote copies, remote signals or barrier semaphores. Data moves between devices by JAX's collectives and lax.ppermute only.
A program may use at most 64 MiB of HBM per device.

```python
import math
import jax
import jax.numpy as jnp
import numpy as np
from jax import lax

NB = 512
ORB_DEV = 768
ATOMS_DEV = 4
ATOM_MOST = 256
ROUNDS = 2
DEGREE = 8
ROTS = 4
NORB = 6144
N_ATOMS = 8


def draw_subspace(key, part):
    key_a, key_b, key_c = jax.random.split(key, 3)
    blocks = NORB // ORB_DEV
    noise_vals = jnp.clip(jax.random.normal(key_a, (NB, NORB), jnp.float32), -4.0, 4.0)
    row_scale = jnp.exp(jnp.log(10.0) * jax.random.uniform(key_b, (1, NORB), jnp.float32))
    col_scale = jnp.exp(jnp.log(10.0) * jax.random.uniform(key_c, (NB, 1), jnp.float32))
    partition = (jnp.arange(NORB, dtype=jnp.int32) // ORB_DEV).astype(jnp.float32)
    trend_scale = jnp.exp(jnp.log(3.0) * partition / max(blocks - 1, 1))
    return (0.1 * noise_vals * row_scale * col_scale * trend_scale[None, :]).astype(jnp.bfloat16)


def touch_ends(values, own_key, least, largest):
    extent = values.shape
    spot = [jax.random.randint(jax.random.fold_in(own_key, axis), (), 0, extent[axis]) for axis in range(len(extent))]
    values = values.at[tuple(spot)].set(least)
    longest = extent.index(max(extent))
    spot[longest] = (spot[longest] + 1) % extent[longest]
    return values.at[tuple(spot)].set(largest)


def block_levels(own_key, shape, shards, least, top_value):
    factor_of, own = 1.0, jax.random.fold_in(own_key, 6)
    for axis_at, parts in shards:
        heights = jnp.exp(jax.random.uniform(jax.random.fold_in(own, axis_at), (parts,), jnp.float32, least / len(shards), top_value / len(shards)))
        factor_of = factor_of * jnp.repeat(heights, shape[axis_at] // parts).reshape([-1 if axis == axis_at else 1 for axis in range(len(shape))])
    return factor_of


def length_profile(number_of, total, bound, slope):
    portions = [(1 << 20) // math.isqrt(standing ** slope) + 1 for standing in range(2, number_of + 1)]
    surplus, counts = total - bound - (number_of - 1), [1] * (number_of - 1)
    while surplus > 0:
        movable = [i for i in range(number_of - 1) if counts[i] < bound]
        mass, remaining = sum([portions[i] for i in movable]), surplus
        for i in movable:
            extra = min(bound - counts[i], max(1, remaining * portions[i] // mass), surplus)
            counts[i] = counts[i] + extra
            surplus = surplus - extra
    return np.array([bound] + counts)


def ragged(key, number_of, total, most, slope):
    if number_of == 2:
        one = jax.random.randint(key, (), max(1, total - most), min(most, total - 1) + 1)
        return jnp.stack([one, total - one])
    tallies = jnp.asarray(length_profile(number_of, total, most, slope), jnp.int32)
    pairs = (number_of - 1) // 2
    source_of, receiver = tallies[1:1 + 2 * pairs:2], tallies[2:2 + 2 * pairs:2]
    room = jnp.minimum(source_of - 1, most - receiver)
    passed = jax.random.randint(jax.random.fold_in(key, 1), (pairs,), 0, 1 << 20) % (room + 1)
    tallies = tallies.at[1:1 + 2 * pairs:2].set(source_of - passed).at[2:2 + 2 * pairs:2].set(receiver + passed)
    return tallies[jax.random.permutation(jax.random.fold_in(key, 2), number_of)]


def bell_draw(key, shape, spread, limit, cuts=(), held_as=jnp.bfloat16):
    drawn = jax.random.normal(key, shape, jnp.float32) * spread
    if len(cuts) > 0:
        drawn = block_levels(key, shape, cuts, -0.22, 0.18) * drawn
    return jnp.clip(drawn, min=-limit, max=limit).astype(held_as)


def setup_inputs(seed: int = 0) -> dict:
    key_list = jax.random.split(jax.random.key(seed), 7)
    return {
        "subspace": draw_subspace(jax.random.fold_in(key_list[6], 71), 0),
        "diag_block": bell_draw(key_list[1], (NORB, ORB_DEV), (10 * ORB_DEV) ** -0.5, 0.0625, ((0, 8),)),
        "pair_block": bell_draw(key_list[2], (ROUNDS, NORB, ORB_DEV), (10 * ORB_DEV) ** -0.5, 0.0625, ((1, 8),)),
        "pair_pattern": touch_ends((jax.random.randint(key_list[3], (ROUNDS, ATOMS_DEV * N_ATOMS, ATOMS_DEV), 0, 4) < 3).astype(jnp.int32), jax.random.fold_in(key_list[3], 1), 0, 1),
        "atom_sizes": jax.vmap(lambda own: ragged(own, ATOMS_DEV, ORB_DEV, ATOM_MOST, 2))(jax.random.split(key_list[4], N_ATOMS)).reshape((N_ATOMS, ATOMS_DEV)).astype(jnp.int32),
        "rotations": bell_draw(key_list[5], (ROTS, NB, NB), NB ** -0.5, 0.25, ((2, 4),)),
    }


filter_center = 0.1
filter_half = 1.25
norm_eps = 1e-06

def atom_onehot(atom_counts, length_total):
    atom_ends = jnp.cumsum(atom_counts, axis=-1).astype(jnp.int32)
    atom_starts = (atom_ends - atom_counts).astype(jnp.int32)
    positions = jnp.arange(length_total, dtype=jnp.int32)
    inside = (positions >= atom_starts[..., None]) & (positions < atom_ends[..., None])
    return inside.astype(jnp.float32)

def diagonal_weights(onehot_rows):
    levels = jnp.arange(onehot_rows.shape[0], dtype=jnp.float32)
    atom_index = lax.optimization_barrier(jnp.sum(onehot_rows * levels[:, None], axis=0))
    upper_flag = (atom_index[:, None] < atom_index[None, :]).astype(jnp.float32)
    same_atom = (atom_index[:, None] == atom_index[None, :]).astype(jnp.float32)
    return upper_flag + 0.5 * same_atom

def build_blocks(diag_block, pair_block, pair_pattern, atom_sizes):
    count_parts = atom_sizes.shape[0]
    onehot_all = atom_onehot(atom_sizes, ORB_DEV)
    diag_full = diag_block.reshape(count_parts, ORB_DEV, ORB_DEV).astype(jnp.float32)
    upper_part = diag_full * jax.vmap(diagonal_weights)(onehot_all)
    diag_sym = (upper_part + jnp.swapaxes(upper_part, 1, 2)).astype(jnp.bfloat16)
    parts_index = jnp.arange(count_parts, dtype=jnp.int32)
    pair_list = []
    for round_index in range(ROUNDS):
        partner = jnp.bitwise_xor(parts_index, 1 << round_index)
        pattern = pair_pattern[round_index].reshape(count_parts, ATOMS_DEV, ATOMS_DEV).astype(jnp.float32)
        right_side = jnp.einsum('pab,pbj->paj', pattern, onehot_all[partner])
        pair_mask = jnp.einsum('pai,paj->pij', onehot_all, right_side)
        pair_mat = pair_block[round_index].reshape(count_parts, ORB_DEV, ORB_DEV).astype(jnp.float32) * pair_mask
        pair_list.append(pair_mat.astype(jnp.bfloat16))
    return (diag_sym, pair_list)

def apply_operator(values, diag_sym, pair_list):
    count_parts = diag_sym.shape[0]
    band_rows = values.reshape(NB, count_parts, ORB_DEV).transpose(1, 0, 2).astype(jnp.float32)
    result = jnp.einsum('pbj,pji->pbi', band_rows, diag_sym.astype(jnp.float32))
    parts_index = jnp.arange(count_parts, dtype=jnp.int32)
    for round_index in range(ROUNDS):
        partner = jnp.bitwise_xor(parts_index, 1 << round_index)
        pair_mat = pair_list[round_index].astype(jnp.float32)
        own_term = jnp.einsum('pbj,pij->pbi', band_rows[partner], pair_mat)
        theirs = jnp.einsum('pbi,pij->pbj', band_rows, pair_mat)
        result = result + own_term + theirs[partner]
    return result.transpose(1, 0, 2).reshape(NB, count_parts * ORB_DEV)

def reference(subspace, diag_block, pair_block, pair_pattern, atom_sizes, rotations):
    diag_sym, pair_list = build_blocks(diag_block, pair_block, pair_pattern, atom_sizes)
    previous = subspace.astype(jnp.float32)
    current = (apply_operator(subspace, diag_sym, pair_list) - filter_center * previous) / filter_half
    for degree_index in range(1, DEGREE):
        applied = apply_operator(current.astype(jnp.bfloat16), diag_sym, pair_list)
        following = 2.0 * (applied - filter_center * current) / filter_half - previous
        previous, current = (current, following)
    basis_rows = current
    for rotation_index in range(ROTS):
        rounded = basis_rows.astype(jnp.bfloat16)
        mixed_rows = jnp.dot(rotations[rotation_index].T, rounded, preferred_element_type=jnp.float32)
        col_norm = jnp.sqrt(lax.optimization_barrier(jnp.sum(mixed_rows * mixed_rows, axis=1)) / mixed_rows.shape[1] + norm_eps)
        basis_rows = mixed_rows / col_norm[:, None]
    return basis_rows
```

```python
import jax
import jax.numpy as jnp
from jax import lax
from jax.sharding import PartitionSpec as P

ROUNDS = 2
DEGREE = 8
ROTS = 4


filter_center = 0.1
filter_half = 1.25
norm_eps = 1e-06


def swapped(value, axis, stride):
    mask = 2**stride
    pairs = [(source, source ^ mask) for source in range(lax.axis_size(axis))]
    return lax.ppermute(value, axis, pairs)


def gather_bands(value):
    count = lax.axis_size("bands")
    here = lax.axis_index("bands")
    pieces = [value]
    for shift in range(1, count):
        pairs = [(source, (source + shift) % count) for source in range(count)]
        pieces.append(lax.ppermute(value, "bands", pairs))
    order = (here - jnp.arange(count, dtype=jnp.int32)) % count
    return jnp.take(jnp.stack(pieces), order, axis=0)


def atoms_sum(value):
    count = lax.axis_size("atoms")
    stride = 0
    while (1 << stride) < count:
        value = value + swapped(value, "atoms", stride)
        stride += 1
    return value


def atom_onehot(atom_counts, length_total):
    atom_ends = jnp.cumsum(atom_counts, axis=-1)
    atom_starts = atom_ends - atom_counts
    positions = jnp.arange(length_total, dtype=jnp.int32)
    inside = (positions >= atom_starts[..., None]) & (positions < atom_ends[..., None])
    return inside.astype(jnp.float32)


def diagonal_weights(onehot_rows):
    levels = jnp.arange(onehot_rows.shape[0], dtype=jnp.float32)
    atom_index = jnp.sum(onehot_rows * levels[:, None], axis=0)
    upper_flag = (atom_index[:, None] < atom_index[None, :]).astype(jnp.float32)
    same_atom = (atom_index[:, None] == atom_index[None, :]).astype(jnp.float32)
    return upper_flag + 0.5 * same_atom


def apply_operator(values, diag_sym, coupling):
    result = jnp.dot(values, diag_sym, preferred_element_type=jnp.float32)
    for round_index in range(ROUNDS):
        pair_mat = coupling[round_index]
        other_rows = swapped(values, "atoms", round_index)
        own_term = lax.dot_general(
            other_rows, pair_mat, (((1,), (1,)), ((), ())), preferred_element_type=jnp.float32
        )
        sent_term = jnp.dot(values, pair_mat, preferred_element_type=jnp.float32)
        returned = swapped(sent_term.astype(jnp.bfloat16), "atoms", round_index).astype(
            sent_term.dtype
        )
        result = result + own_term + returned
    return result


def body(subspace, diag_block, pair_block, pair_pattern, atom_sizes, rotations):
    orb_dev = diag_block.shape[1]
    atoms_here = lax.axis_index("atoms")
    onehot_own = atom_onehot(
        lax.dynamic_index_in_dim(atom_sizes, atoms_here, 0, keepdims=False), orb_dev
    )
    upper_part = diag_block.astype(jnp.float32) * diagonal_weights(onehot_own)
    diag_sym = (upper_part + upper_part.T).astype(jnp.bfloat16)
    coupling = []
    for round_index in range(ROUNDS):
        partner = jnp.bitwise_xor(atoms_here, 1 << round_index)
        onehot_other = atom_onehot(
            lax.dynamic_index_in_dim(atom_sizes, partner, 0, keepdims=False), orb_dev
        )
        pattern = pair_pattern[round_index].astype(jnp.float32)
        right_side = jnp.dot(pattern, onehot_other, precision=lax.Precision.HIGHEST)
        pair_mask = lax.dot_general(
            onehot_own, right_side, (((0,), (0,)), ((), ())), precision=lax.Precision.HIGHEST
        )
        pair_mat = (pair_block[round_index].astype(jnp.float32) * pair_mask).astype(jnp.bfloat16)
        coupling.append(pair_mat)
    previous = subspace.astype(jnp.float32)
    current = (
        apply_operator(subspace, diag_sym, coupling) - filter_center * previous
    ) / filter_half
    for degree_index in range(1, DEGREE):
        applied = apply_operator(current.astype(jnp.bfloat16), diag_sym, coupling)
        following = 2.0 * (applied - filter_center * current) / filter_half - previous
        previous, current = (current, following)
    total_orbitals = orb_dev * lax.axis_size("atoms")
    band_count = lax.axis_size("bands")
    local_bands = current.shape[0]
    rot_steps, all_bands, _ = rotations.shape
    full_rot = gather_bands(rotations)
    full_rot = jnp.transpose(full_rot, (1, 2, 0, 3)).reshape(rot_steps, all_bands, all_bands)
    basis_all = gather_bands(current.astype(jnp.bfloat16)).reshape(all_bands, orb_dev)
    for rotation_index in range(ROTS - 1):
        mixed_rows = lax.dot_general(
            full_rot[rotation_index],
            basis_all,
            (((0,), (0,)), ((), ())),
            preferred_element_type=jnp.float32,
        )
        squares = atoms_sum(jnp.sum(mixed_rows * mixed_rows, axis=1))
        col_norm = jnp.sqrt(squares / total_orbitals + norm_eps)
        basis_all = (mixed_rows / col_norm[:, None]).astype(jnp.bfloat16)
    mixed_rows = lax.dot_general(
        rotations[ROTS - 1],
        basis_all,
        (((0,), (0,)), ((), ())),
        preferred_element_type=jnp.float32,
    )
    squares = atoms_sum(jnp.sum(mixed_rows * mixed_rows, axis=1))
    col_norm = jnp.sqrt(squares / total_orbitals + norm_eps)
    return mixed_rows / col_norm[:, None]


def solution(mesh):
    placed = (
        P("bands", "atoms"),
        P("atoms", None),
        P(None, "atoms", None),
        P(None, "atoms", None),
        P(),
        P(None, None, "bands"),
    )
    return jax.shard_map(
        body, mesh=mesh, in_specs=placed, out_specs=P("bands", "atoms"), check_vma=False
    )
```

```python
import jax
import jax.numpy as jnp
from jax import lax
from jax.sharding import PartitionSpec as P

ROUNDS = 2
DEGREE = 8
ROTS = 4
PAD_ROWS = 16


filter_center = 0.1
filter_half = 1.25
norm_eps = 1e-06


def swapped(value, axis, stride):
    mask = 2**stride
    pairs = [(source, source ^ mask) for source in range(lax.axis_size(axis))]
    return lax.ppermute(value, axis, pairs)


def gather_bands(value):
    count = lax.axis_size("bands")
    here = lax.axis_index("bands")
    pieces = [value]
    for shift in range(1, count):
        pairs = [(source, (source + shift) % count) for source in range(count)]
        pieces.append(lax.ppermute(value, "bands", pairs))
    order = (here - jnp.arange(count, dtype=jnp.int32)) % count
    return jnp.take(jnp.stack(pieces), order, axis=0)


def atoms_sum(value):
    count = lax.axis_size("atoms")
    stride = 0
    while (1 << stride) < count:
        value = value + swapped(value, "atoms", stride)
        stride += 1
    return value


def atom_index(atom_counts, length_total):
    atom_ends = jnp.cumsum(atom_counts)
    positions = jnp.arange(length_total, dtype=jnp.int32)
    return jnp.sum((positions[:, None] >= atom_ends[None, :]).astype(jnp.int32), axis=1)


def pattern_mask(pattern, row_atoms, col_atoms):
    atoms_dev = pattern.shape[0]
    col_onehot = (col_atoms[None, :] == jnp.arange(atoms_dev, dtype=jnp.int32)[:, None])
    per_row = jnp.dot(
        pattern.astype(jnp.float32), col_onehot.astype(jnp.float32), precision=lax.Precision.HIGHEST
    )
    mask = jnp.broadcast_to(per_row[0][None, :], (row_atoms.shape[0], col_atoms.shape[0]))
    for atom in range(1, atoms_dev):
        mask = jnp.where((row_atoms == atom)[:, None], per_row[atom][None, :], mask)
    return mask > 0.5


def body(subspace, diag_block, pair_block, pair_pattern, atom_sizes, rotations):
    orb_dev = diag_block.shape[1]
    atoms_dev = pair_pattern.shape[2]
    atoms_here = lax.axis_index("atoms")
    shipped = []
    for round_index in range(ROUNDS):
        pattern_rows = jnp.zeros((PAD_ROWS, orb_dev), jnp.bfloat16)
        pattern_rows = lax.dynamic_update_slice(
            pattern_rows, pair_pattern[round_index].astype(jnp.bfloat16), (0, 0)
        )
        packed = jnp.concatenate([pair_block[round_index], pattern_rows], axis=0)
        shipped.append(swapped(packed, "atoms", round_index))
    full_rot = gather_bands(rotations)
    own_atoms = atom_index(
        lax.dynamic_index_in_dim(atom_sizes, atoms_here, 0, keepdims=False), orb_dev
    )
    upper_flag = (own_atoms[:, None] < own_atoms[None, :]).astype(jnp.float32)
    same_atom = (own_atoms[:, None] == own_atoms[None, :]).astype(jnp.float32)
    upper_part = diag_block.astype(jnp.float32) * (upper_flag + 0.5 * same_atom)
    diag_sym = (upper_part + upper_part.T).astype(jnp.bfloat16)
    own_pair_t = []
    other_pair = []
    for round_index in range(ROUNDS):
        partner = jnp.bitwise_xor(atoms_here, 1 << round_index)
        other_atoms = atom_index(
            lax.dynamic_index_in_dim(atom_sizes, partner, 0, keepdims=False), orb_dev
        )
        own_mask = pattern_mask(pair_pattern[round_index], own_atoms, other_atoms)
        own_pair = jnp.where(own_mask, pair_block[round_index], jnp.zeros((), jnp.bfloat16))
        own_pair_t.append(own_pair.T)
        received = shipped[round_index]
        other_pattern = received[orb_dev : orb_dev + atoms_dev, :atoms_dev]
        other_mask = pattern_mask(other_pattern, other_atoms, own_atoms)
        other_pair.append(
            jnp.where(other_mask, received[:orb_dev], jnp.zeros((), jnp.bfloat16))
        )

    def apply_operator(values):
        result = jnp.dot(values, diag_sym, preferred_element_type=jnp.float32)
        for round_index in range(ROUNDS):
            other_rows = swapped(values, "atoms", round_index)
            result = result + jnp.dot(
                other_rows, own_pair_t[round_index], preferred_element_type=jnp.float32
            )
            result = result + jnp.dot(
                other_rows, other_pair[round_index], preferred_element_type=jnp.float32
            )
        return result

    previous = subspace.astype(jnp.float32)
    current = (apply_operator(subspace) - filter_center * previous) / filter_half
    for degree_index in range(1, DEGREE):
        applied = apply_operator(current.astype(jnp.bfloat16))
        following = 2.0 * (applied - filter_center * current) / filter_half - previous
        previous, current = (current, following)
    total_orbitals = orb_dev * lax.axis_size("atoms")
    rot_steps, all_bands, _ = rotations.shape
    full_rot = jnp.transpose(full_rot, (1, 2, 0, 3)).reshape(rot_steps, all_bands, all_bands)
    basis_all = gather_bands(current.astype(jnp.bfloat16)).reshape(all_bands, orb_dev)
    for rotation_index in range(ROTS - 1):
        mixed_rows = lax.dot_general(
            full_rot[rotation_index],
            basis_all,
            (((0,), (0,)), ((), ())),
            preferred_element_type=jnp.float32,
        )
        squares = atoms_sum(jnp.sum(mixed_rows * mixed_rows, axis=1))
        col_norm = jnp.sqrt(squares / total_orbitals + norm_eps)
        basis_all = (mixed_rows / col_norm[:, None]).astype(jnp.bfloat16)
    mixed_rows = lax.dot_general(
        rotations[ROTS - 1],
        basis_all,
        (((0,), (0,)), ((), ())),
        preferred_element_type=jnp.float32,
    )
    squares = atoms_sum(jnp.sum(mixed_rows * mixed_rows, axis=1))
    col_norm = jnp.sqrt(squares / total_orbitals + norm_eps)
    return mixed_rows / col_norm[:, None]


def solution(mesh):
    placed = (
        P("bands", "atoms"),
        P("atoms", None),
        P(None, "atoms", None),
        P(None, "atoms", None),
        P(),
        P(None, None, "bands"),
    )
    return jax.shard_map(
        body, mesh=mesh, in_specs=placed, out_specs=P("bands", "atoms"), check_vma=False
    )
```

```python
import jax
import jax.numpy as jnp
from jax import lax
from jax.sharding import PartitionSpec as P

ROUNDS = 2
DEGREE = 8
ROTS = 4
PAD_ROWS = 16


filter_center = 0.1
filter_half = 1.25
norm_eps = 1e-06


def swapped(value, axis, stride):
    mask = 2**stride
    pairs = [(source, source ^ mask) for source in range(lax.axis_size(axis))]
    return lax.ppermute(value, axis, pairs)


def gather_bands(value):
    count = lax.axis_size("bands")
    here = lax.axis_index("bands")
    pieces = [value]
    for shift in range(1, count):
        pairs = [(source, (source + shift) % count) for source in range(count)]
        pieces.append(lax.ppermute(value, "bands", pairs))
    order = (here - jnp.arange(count, dtype=jnp.int32)) % count
    return jnp.take(jnp.stack(pieces), order, axis=0)


def atoms_sum(value):
    count = lax.axis_size("atoms")
    stride = 0
    while (1 << stride) < count:
        value = value + swapped(value, "atoms", stride)
        stride += 1
    return value


def atom_index(atom_counts, length_total):
    atom_ends = jnp.cumsum(atom_counts)
    positions = jnp.arange(length_total, dtype=jnp.int32)
    return jnp.sum((positions[:, None] >= atom_ends[None, :]).astype(jnp.int32), axis=1)


def pattern_mask(pattern, row_atoms, col_atoms):
    levels = jnp.arange(pattern.shape[0], dtype=jnp.int32)
    row_onehot = (row_atoms[:, None] == levels[None, :]).astype(jnp.bfloat16)
    col_onehot = (col_atoms[:, None] == levels[None, :]).astype(jnp.bfloat16)
    per_row = jnp.dot(row_onehot, pattern.astype(jnp.bfloat16), preferred_element_type=jnp.float32)
    mask = lax.dot_general(
        per_row.astype(jnp.bfloat16), col_onehot, (((1,), (1,)), ((), ())),
        preferred_element_type=jnp.float32,
    )
    return mask > 0.5


def body(subspace, diag_block, pair_block, pair_pattern, atom_sizes, rotations):
    orb_dev = diag_block.shape[1]
    atoms_dev = pair_pattern.shape[2]
    atoms_here = lax.axis_index("atoms")
    shipped = []
    for round_index in range(ROUNDS):
        pattern_rows = jnp.zeros((PAD_ROWS, orb_dev), jnp.bfloat16)
        pattern_rows = lax.dynamic_update_slice(
            pattern_rows, pair_pattern[round_index].astype(jnp.bfloat16), (0, 0)
        )
        packed = jnp.concatenate([pair_block[round_index], pattern_rows], axis=0)
        shipped.append(swapped(packed, "atoms", round_index))
    full_rot = gather_bands(rotations)
    own_atoms = atom_index(
        lax.dynamic_index_in_dim(atom_sizes, atoms_here, 0, keepdims=False), orb_dev
    )
    upper_flag = (own_atoms[:, None] < own_atoms[None, :]).astype(jnp.float32)
    same_atom = (own_atoms[:, None] == own_atoms[None, :]).astype(jnp.float32)
    upper_part = diag_block.astype(jnp.float32) * (upper_flag + 0.5 * same_atom)
    diag_sym = (upper_part + upper_part.T).astype(jnp.bfloat16)
    own_pair_t = []
    other_pair = []
    for round_index in range(ROUNDS):
        partner = jnp.bitwise_xor(atoms_here, 1 << round_index)
        other_atoms = atom_index(
            lax.dynamic_index_in_dim(atom_sizes, partner, 0, keepdims=False), orb_dev
        )
        own_mask = pattern_mask(pair_pattern[round_index], own_atoms, other_atoms)
        own_pair = jnp.where(own_mask, pair_block[round_index], jnp.zeros((), jnp.bfloat16))
        own_pair_t.append(own_pair)
        received = shipped[round_index]
        other_pattern = received[orb_dev : orb_dev + atoms_dev, :atoms_dev]
        other_mask = pattern_mask(other_pattern, other_atoms, own_atoms)
        other_pair.append(
            jnp.where(other_mask, received[:orb_dev], jnp.zeros((), jnp.bfloat16))
        )

    def apply_operator(values):
        result = jnp.dot(values, diag_sym, preferred_element_type=jnp.float32)
        for round_index in range(ROUNDS):
            other_rows = swapped(values, "atoms", round_index)
            result = result + lax.dot_general(
                other_rows, own_pair_t[round_index], (((1,), (1,)), ((), ())),
                preferred_element_type=jnp.float32,
            )
            result = result + jnp.dot(
                other_rows, other_pair[round_index], preferred_element_type=jnp.float32
            )
        return result

    def chebyshev(start_rows):
        previous = start_rows.astype(jnp.float32)
        current = (apply_operator(start_rows) - filter_center * previous) / filter_half
        for degree_index in range(1, DEGREE):
            applied = apply_operator(current.astype(jnp.bfloat16))
            following = 2.0 * (applied - filter_center * current) / filter_half - previous
            previous, current = (current, following)
        return current

    half_bands = subspace.shape[0] // 2
    current = jnp.concatenate(
        [chebyshev(subspace[:half_bands]), chebyshev(subspace[half_bands:])], axis=0
    )
    total_orbitals = orb_dev * lax.axis_size("atoms")
    rot_steps, all_bands, _ = rotations.shape
    full_rot = jnp.transpose(full_rot, (1, 2, 0, 3)).reshape(rot_steps, all_bands, all_bands)
    basis_all = gather_bands(current.astype(jnp.bfloat16)).reshape(all_bands, orb_dev)
    for rotation_index in range(ROTS - 1):
        mixed_rows = lax.dot_general(
            full_rot[rotation_index],
            basis_all,
            (((0,), (0,)), ((), ())),
            preferred_element_type=jnp.float32,
        )
        squares = atoms_sum(jnp.sum(mixed_rows * mixed_rows, axis=1))
        col_norm = jnp.sqrt(squares / total_orbitals + norm_eps)
        basis_all = (mixed_rows / col_norm[:, None]).astype(jnp.bfloat16)
    mixed_rows = lax.dot_general(
        rotations[ROTS - 1],
        basis_all,
        (((0,), (0,)), ((), ())),
        preferred_element_type=jnp.float32,
    )
    squares = atoms_sum(jnp.sum(mixed_rows * mixed_rows, axis=1))
    col_norm = jnp.sqrt(squares / total_orbitals + norm_eps)
    return mixed_rows / col_norm[:, None]


def solution(mesh):
    placed = (
        P("bands", "atoms"),
        P("atoms", None),
        P(None, "atoms", None),
        P(None, "atoms", None),
        P(),
        P(None, None, "bands"),
    )
    return jax.shard_map(
        body, mesh=mesh, in_specs=placed, out_specs=P("bands", "atoms"), check_vma=False
    )
```

```python
import jax
import jax.numpy as jnp
from jax import lax
from jax.sharding import PartitionSpec as P

ROUNDS = 2
DEGREE = 8
ROTS = 4
GATHER_AT = 2


filter_center = 0.1
filter_half = 1.25
norm_eps = 1e-06


def swapped(value, axis, stride):
    mask = 2**stride
    pairs = [(source, source ^ mask) for source in range(lax.axis_size(axis))]
    return lax.ppermute(value, axis, pairs)


def gather_bands(value):
    count = lax.axis_size("bands")
    here = lax.axis_index("bands")
    pieces = [value]
    for shift in range(1, count):
        pairs = [(source, (source + shift) % count) for source in range(count)]
        pieces.append(lax.ppermute(value, "bands", pairs))
    order = (here - jnp.arange(count, dtype=jnp.int32)) % count
    return jnp.take(jnp.stack(pieces), order, axis=0)


def gather_pieces(value):
    count = lax.axis_size("bands")
    pieces = [value]
    for shift in range(1, count):
        pairs = [(source, (source + shift) % count) for source in range(count)]
        pieces.append(lax.ppermute(value, "bands", pairs))
    return jnp.stack(pieces)


def atoms_sum(value):
    count = lax.axis_size("atoms")
    stride = 0
    while (1 << stride) < count:
        value = value + swapped(value, "atoms", stride)
        stride += 1
    return value


def atom_index(atom_counts, length_total):
    atom_ends = jnp.cumsum(atom_counts)
    positions = jnp.arange(length_total, dtype=jnp.int32)
    return jnp.sum((positions[:, None] >= atom_ends[None, :]).astype(jnp.int32), axis=1)


def pattern_mask(pattern, row_atoms, col_atoms):
    levels = jnp.arange(pattern.shape[0], dtype=jnp.int32)
    row_onehot = (row_atoms[:, None] == levels[None, :]).astype(jnp.bfloat16)
    col_onehot = (col_atoms[:, None] == levels[None, :]).astype(jnp.bfloat16)
    per_row = jnp.dot(row_onehot, pattern.astype(jnp.bfloat16), preferred_element_type=jnp.float32)
    mask = lax.dot_general(
        per_row.astype(jnp.bfloat16), col_onehot, (((1,), (1,)), ((), ())),
        preferred_element_type=jnp.float32,
    )
    return mask > 0.5


def body(subspace, diag_block, pair_block, pair_pattern, atom_sizes, rotations):
    orb_dev = diag_block.shape[1]
    atoms_dev = pair_pattern.shape[2]
    atoms_here = lax.axis_index("atoms")
    shipped = [swapped(pair_block[r], "atoms", r) for r in range(ROUNDS)]
    shipped_pattern = [swapped(pair_pattern[r], "atoms", r) for r in range(ROUNDS)]
    own_atoms = atom_index(
        lax.dynamic_index_in_dim(atom_sizes, atoms_here, 0, keepdims=False), orb_dev
    )
    upper_flag = (own_atoms[:, None] < own_atoms[None, :]).astype(jnp.float32)
    same_atom = (own_atoms[:, None] == own_atoms[None, :]).astype(jnp.float32)
    upper_part = diag_block.astype(jnp.float32) * (upper_flag + 0.5 * same_atom)
    diag_sym = (upper_part + upper_part.T).astype(jnp.bfloat16)
    own_pair_t = []
    other_pair = []
    for round_index in range(ROUNDS):
        partner = jnp.bitwise_xor(atoms_here, 1 << round_index)
        other_atoms = atom_index(
            lax.dynamic_index_in_dim(atom_sizes, partner, 0, keepdims=False), orb_dev
        )
        own_mask = pattern_mask(pair_pattern[round_index], own_atoms, other_atoms)
        own_pair = jnp.where(own_mask, pair_block[round_index], jnp.zeros((), jnp.bfloat16))
        own_pair_t.append(own_pair)
        other_mask = pattern_mask(shipped_pattern[round_index], other_atoms, own_atoms)
        other_pair.append(
            jnp.where(other_mask, shipped[round_index], jnp.zeros((), jnp.bfloat16))
        )

    def apply_operator(values):
        result = jnp.dot(values, diag_sym, preferred_element_type=jnp.float32)
        for round_index in range(ROUNDS):
            other_rows = swapped(values, "atoms", round_index)
            result = result + lax.dot_general(
                other_rows, own_pair_t[round_index], (((1,), (1,)), ((), ())),
                preferred_element_type=jnp.float32,
            )
            result = result + jnp.dot(
                other_rows, other_pair[round_index], preferred_element_type=jnp.float32
            )
        return result

    def chebyshev(start_rows, hook):
        previous = start_rows.astype(jnp.float32)
        current = (apply_operator(start_rows) - filter_center * previous) / filter_half
        for degree_index in range(1, DEGREE):
            if degree_index == GATHER_AT:
                current = hook(current)
            applied = apply_operator(current.astype(jnp.bfloat16))
            following = 2.0 * (applied - filter_center * current) / filter_half - previous
            previous, current = (current, following)
        return current

    gathered = []

    def start_rotation_gather(current):
        held, current = lax.optimization_barrier((rotations[: ROTS - 1], current))
        gathered.append(gather_pieces(held))
        return current

    half_bands = subspace.shape[0] // 2
    current = jnp.concatenate(
        [
            chebyshev(subspace[:half_bands], start_rotation_gather),
            chebyshev(subspace[half_bands:], lambda rows: rows),
        ],
        axis=0,
    )
    rot_pieces = gathered[0]
    total_orbitals = orb_dev * lax.axis_size("atoms")
    band_count = lax.axis_size("bands")
    band_here = lax.axis_index("bands")
    all_bands = rotations.shape[1]
    basis_all = gather_bands(current.astype(jnp.bfloat16)).reshape(all_bands, orb_dev)
    for rotation_index in range(ROTS - 1):
        groups = []
        for group in range(band_count):
            piece = lax.dynamic_index_in_dim(
                rot_pieces, (band_here - group) % band_count, 0, keepdims=False
            )
            groups.append(
                lax.dot_general(
                    piece[rotation_index],
                    basis_all,
                    (((0,), (0,)), ((), ())),
                    preferred_element_type=jnp.float32,
                )
            )
        mixed_rows = jnp.concatenate(groups, axis=0)
        squares = atoms_sum(jnp.sum(mixed_rows * mixed_rows, axis=1))
        col_norm = jnp.sqrt(squares / total_orbitals + norm_eps)
        basis_all = (mixed_rows / col_norm[:, None]).astype(jnp.bfloat16)
    mixed_rows = lax.dot_general(
        rotations[ROTS - 1],
        basis_all,
        (((0,), (0,)), ((), ())),
        preferred_element_type=jnp.float32,
    )
    squares = atoms_sum(jnp.sum(mixed_rows * mixed_rows, axis=1))
    col_norm = jnp.sqrt(squares / total_orbitals + norm_eps)
    return mixed_rows / col_norm[:, None]


def solution(mesh):
    placed = (
        P("bands", "atoms"),
        P("atoms", None),
        P(None, "atoms", None),
        P(None, "atoms", None),
        P(),
        P(None, None, "bands"),
    )
    return jax.shard_map(
        body, mesh=mesh, in_specs=placed, out_specs=P("bands", "atoms"), check_vma=False
    )
```

```python
import jax
import jax.numpy as jnp
from jax import lax
from jax.sharding import PartitionSpec as P

ROUNDS = 2
DEGREE = 8
ROTS = 4
GATHER_AT = 1


filter_center = 0.1
filter_half = 1.25
norm_eps = 1e-06


def swapped(value, axis, stride):
    mask = 2**stride
    pairs = [(source, source ^ mask) for source in range(lax.axis_size(axis))]
    return lax.ppermute(value, axis, pairs)


def gather_bands(value):
    count = lax.axis_size("bands")
    here = lax.axis_index("bands")
    pieces = [value]
    for shift in range(1, count):
        pairs = [(source, (source + shift) % count) for source in range(count)]
        pieces.append(lax.ppermute(value, "bands", pairs))
    order = (here - jnp.arange(count, dtype=jnp.int32)) % count
    return jnp.take(jnp.stack(pieces), order, axis=0)


def gather_pieces(value):
    count = lax.axis_size("bands")
    pieces = [value]
    for shift in range(1, count):
        pairs = [(source, (source + shift) % count) for source in range(count)]
        pieces.append(lax.ppermute(value, "bands", pairs))
    return jnp.stack(pieces)


def atoms_sum(value):
    count = lax.axis_size("atoms")
    stride = 0
    while (1 << stride) < count:
        value = value + swapped(value, "atoms", stride)
        stride += 1
    return value


def atom_index(atom_counts, length_total):
    atom_ends = jnp.cumsum(atom_counts)
    positions = jnp.arange(length_total, dtype=jnp.int32)
    return jnp.sum((positions[:, None] >= atom_ends[None, :]).astype(jnp.int32), axis=1)


def pattern_mask(pattern, row_atoms, col_atoms):
    levels = jnp.arange(pattern.shape[0], dtype=jnp.int32)
    row_onehot = (row_atoms[:, None] == levels[None, :]).astype(jnp.bfloat16)
    per_row = jnp.dot(row_onehot, pattern.astype(jnp.bfloat16), preferred_element_type=jnp.float32)
    mask = jnp.broadcast_to(per_row[:, :1], (row_atoms.shape[0], col_atoms.shape[0]))
    for atom in range(1, pattern.shape[1]):
        mask = jnp.where((col_atoms == atom)[None, :], per_row[:, atom : atom + 1], mask)
    return mask > 0.5


def body(subspace, diag_block, pair_block, pair_pattern, atom_sizes, rotations):
    orb_dev = diag_block.shape[1]
    atoms_dev = pair_pattern.shape[2]
    atoms_here = lax.axis_index("atoms")
    shipped = [swapped(pair_block[r], "atoms", r) for r in range(ROUNDS)]
    shipped_pattern = [swapped(pair_pattern[r], "atoms", r) for r in range(ROUNDS)]
    own_atoms = atom_index(
        lax.dynamic_index_in_dim(atom_sizes, atoms_here, 0, keepdims=False), orb_dev
    )
    row_atom = own_atoms[:, None]
    col_atom = own_atoms[None, :]
    weight = (row_atom < col_atom).astype(jnp.float32) + 0.5 * (row_atom == col_atom).astype(jnp.float32)
    weight_t = (col_atom < row_atom).astype(jnp.float32) + 0.5 * (row_atom == col_atom).astype(jnp.float32)
    diag_sym = (
        diag_block.astype(jnp.float32) * weight + diag_block.T.astype(jnp.float32) * weight_t
    ).astype(jnp.bfloat16)
    own_pair_t = []
    other_pair = []
    for round_index in range(ROUNDS):
        partner = jnp.bitwise_xor(atoms_here, 1 << round_index)
        other_atoms = atom_index(
            lax.dynamic_index_in_dim(atom_sizes, partner, 0, keepdims=False), orb_dev
        )
        own_mask = pattern_mask(pair_pattern[round_index], own_atoms, other_atoms)
        own_pair = jnp.where(own_mask, pair_block[round_index], jnp.zeros((), jnp.bfloat16))
        own_pair_t.append(own_pair)
        other_mask = pattern_mask(shipped_pattern[round_index], other_atoms, own_atoms)
        other_pair.append(
            jnp.where(other_mask, shipped[round_index], jnp.zeros((), jnp.bfloat16))
        )

    def apply_operator(values):
        result = jnp.dot(values, diag_sym, preferred_element_type=jnp.float32)
        for round_index in range(ROUNDS):
            other_rows = swapped(values, "atoms", round_index)
            result = result + lax.dot_general(
                other_rows, own_pair_t[round_index], (((1,), (1,)), ((), ())),
                preferred_element_type=jnp.float32,
            )
            result = result + jnp.dot(
                other_rows, other_pair[round_index], preferred_element_type=jnp.float32
            )
        return result

    def chebyshev(start_rows, hook):
        previous = start_rows.astype(jnp.float32)
        current = (apply_operator(start_rows) - filter_center * previous) / filter_half
        for degree_index in range(1, DEGREE):
            if degree_index == GATHER_AT:
                current = hook(current)
            applied = apply_operator(current.astype(jnp.bfloat16))
            following = 2.0 * (applied - filter_center * current) / filter_half - previous
            previous, current = (current, following)
        return current

    gathered = []

    def start_rotation_gather(current):
        held, current = lax.optimization_barrier((rotations[: ROTS - 1], current))
        gathered.append(gather_pieces(held))
        return current

    half_bands = subspace.shape[0] // 2
    current = jnp.concatenate(
        [
            chebyshev(subspace[:half_bands], start_rotation_gather),
            chebyshev(subspace[half_bands:], lambda rows: rows),
        ],
        axis=0,
    )
    rot_pieces = gathered[0]
    total_orbitals = orb_dev * lax.axis_size("atoms")
    band_count = lax.axis_size("bands")
    band_here = lax.axis_index("bands")
    all_bands = rotations.shape[1]
    basis_all = gather_bands(current.astype(jnp.bfloat16)).reshape(all_bands, orb_dev)
    for rotation_index in range(ROTS - 1):
        groups = []
        for group in range(band_count):
            piece = lax.dynamic_index_in_dim(
                rot_pieces, (band_here - group) % band_count, 0, keepdims=False
            )
            groups.append(
                lax.dot_general(
                    piece[rotation_index],
                    basis_all,
                    (((0,), (0,)), ((), ())),
                    preferred_element_type=jnp.float32,
                )
            )
        mixed_rows = jnp.concatenate(groups, axis=0)
        squares = atoms_sum(jnp.sum(mixed_rows * mixed_rows, axis=1))
        col_norm = jnp.sqrt(squares / total_orbitals + norm_eps)
        basis_all = (mixed_rows / col_norm[:, None]).astype(jnp.bfloat16)
    mixed_rows = lax.dot_general(
        rotations[ROTS - 1],
        basis_all,
        (((0,), (0,)), ((), ())),
        preferred_element_type=jnp.float32,
    )
    squares = atoms_sum(jnp.sum(mixed_rows * mixed_rows, axis=1))
    col_norm = jnp.sqrt(squares / total_orbitals + norm_eps)
    return mixed_rows / col_norm[:, None]


def solution(mesh):
    placed = (
        P("bands", "atoms"),
        P("atoms", None),
        P(None, "atoms", None),
        P(None, "atoms", None),
        P(),
        P(None, None, "bands"),
    )
    return jax.shard_map(
        body, mesh=mesh, in_specs=placed, out_specs=P("bands", "atoms"), check_vma=False
    )
```

```python
import jax
import jax.numpy as jnp
from jax import lax
from jax.sharding import PartitionSpec as P

ROUNDS = 2
DEGREE = 8
ROTS = 4
GATHER_AT = 2


filter_center = 0.1
filter_half = 1.25
norm_eps = 1e-06


def swapped(value, axis, stride):
    mask = 2**stride
    pairs = [(source, source ^ mask) for source in range(lax.axis_size(axis))]
    return lax.ppermute(value, axis, pairs)


def gather_bands(value):
    count = lax.axis_size("bands")
    here = lax.axis_index("bands")
    pieces = [value]
    for shift in range(1, count):
        pairs = [(source, (source + shift) % count) for source in range(count)]
        pieces.append(lax.ppermute(value, "bands", pairs))
    order = (here - jnp.arange(count, dtype=jnp.int32)) % count
    return jnp.take(jnp.stack(pieces), order, axis=0)


def gather_pieces(value):
    count = lax.axis_size("bands")
    pieces = [value]
    for shift in range(1, count):
        pairs = [(source, (source + shift) % count) for source in range(count)]
        pieces.append(lax.ppermute(value, "bands", pairs))
    return jnp.stack(pieces)


def atoms_sum(value):
    count = lax.axis_size("atoms")
    stride = 0
    while (1 << stride) < count:
        value = value + swapped(value, "atoms", stride)
        stride += 1
    return value


def atom_index(atom_counts, length_total):
    atom_ends = jnp.cumsum(atom_counts)
    positions = jnp.arange(length_total, dtype=jnp.int32)
    return jnp.sum((positions[:, None] >= atom_ends[None, :]).astype(jnp.int32), axis=1)


def pattern_mask(pattern, row_atoms, col_atoms):
    levels = jnp.arange(pattern.shape[0], dtype=jnp.int32)
    row_onehot = (row_atoms[:, None] == levels[None, :]).astype(jnp.bfloat16)
    per_row = jnp.dot(row_onehot, pattern.astype(jnp.bfloat16), preferred_element_type=jnp.float32)
    mask = jnp.broadcast_to(per_row[:, :1], (row_atoms.shape[0], col_atoms.shape[0]))
    for atom in range(1, pattern.shape[1]):
        mask = jnp.where((col_atoms == atom)[None, :], per_row[:, atom : atom + 1], mask)
    return mask > 0.5


def body(subspace, diag_block, pair_block, pair_pattern, atom_sizes, rotations):
    orb_dev = diag_block.shape[1]
    atoms_dev = pair_pattern.shape[2]
    atoms_here = lax.axis_index("atoms")
    half_bands = subspace.shape[0] // 2
    packed = [
        swapped(jnp.concatenate([subspace[:half_bands], pair_block[r]], axis=0), "atoms", r)
        for r in range(ROUNDS)
    ]
    first_rows = [piece[:half_bands] for piece in packed]
    shipped = [piece[half_bands:] for piece in packed]
    shipped_pattern = [swapped(pair_pattern[r], "atoms", r) for r in range(ROUNDS)]
    own_atoms = atom_index(
        lax.dynamic_index_in_dim(atom_sizes, atoms_here, 0, keepdims=False), orb_dev
    )
    upper_flag = (own_atoms[:, None] < own_atoms[None, :]).astype(jnp.float32)
    same_atom = (own_atoms[:, None] == own_atoms[None, :]).astype(jnp.float32)
    upper_part = diag_block.astype(jnp.float32) * (upper_flag + 0.5 * same_atom)
    diag_sym = (upper_part + upper_part.T).astype(jnp.bfloat16)
    own_pair_t = []
    other_pair = []
    for round_index in range(ROUNDS):
        partner = jnp.bitwise_xor(atoms_here, 1 << round_index)
        other_atoms = atom_index(
            lax.dynamic_index_in_dim(atom_sizes, partner, 0, keepdims=False), orb_dev
        )
        own_mask = pattern_mask(pair_pattern[round_index], own_atoms, other_atoms)
        own_pair = jnp.where(own_mask, pair_block[round_index], jnp.zeros((), jnp.bfloat16))
        own_pair_t.append(own_pair)
        other_mask = pattern_mask(shipped_pattern[round_index], other_atoms, own_atoms)
        other_pair.append(
            jnp.where(other_mask, shipped[round_index], jnp.zeros((), jnp.bfloat16))
        )

    def apply_operator(values, received=None):
        result = jnp.dot(values, diag_sym, preferred_element_type=jnp.float32)
        for round_index in range(ROUNDS):
            if received is None:
                other_rows = swapped(values, "atoms", round_index)
            else:
                other_rows = received[round_index]
            result = result + lax.dot_general(
                other_rows, own_pair_t[round_index], (((1,), (1,)), ((), ())),
                preferred_element_type=jnp.float32,
            )
            result = result + jnp.dot(
                other_rows, other_pair[round_index], preferred_element_type=jnp.float32
            )
        return result

    def chebyshev(start_rows, hook, received=None):
        previous = start_rows.astype(jnp.float32)
        current = (apply_operator(start_rows, received) - filter_center * previous) / filter_half
        for degree_index in range(1, DEGREE):
            if degree_index == GATHER_AT:
                current = hook(current)
            applied = apply_operator(current.astype(jnp.bfloat16))
            following = 2.0 * (applied - filter_center * current) / filter_half - previous
            previous, current = (current, following)
        return current

    gathered = []

    def start_rotation_gather(current):
        held, current = lax.optimization_barrier((rotations[: ROTS - 1], current))
        gathered.append(gather_pieces(held))
        return current

    current = jnp.concatenate(
        [
            chebyshev(subspace[:half_bands], start_rotation_gather, first_rows),
            chebyshev(subspace[half_bands:], lambda rows: rows),
        ],
        axis=0,
    )
    rot_pieces = gathered[0]
    total_orbitals = orb_dev * lax.axis_size("atoms")
    band_count = lax.axis_size("bands")
    band_here = lax.axis_index("bands")
    all_bands = rotations.shape[1]
    basis_all = gather_bands(current.astype(jnp.bfloat16)).reshape(all_bands, orb_dev)
    for rotation_index in range(ROTS - 1):
        groups = []
        for group in range(band_count):
            piece = lax.dynamic_index_in_dim(
                rot_pieces, (band_here - group) % band_count, 0, keepdims=False
            )
            groups.append(
                lax.dot_general(
                    piece[rotation_index],
                    basis_all,
                    (((0,), (0,)), ((), ())),
                    preferred_element_type=jnp.float32,
                )
            )
        mixed_rows = jnp.concatenate(groups, axis=0)
        squares = atoms_sum(jnp.sum(mixed_rows * mixed_rows, axis=1))
        col_norm = jnp.sqrt(squares / total_orbitals + norm_eps)
        basis_all = (mixed_rows / col_norm[:, None]).astype(jnp.bfloat16)
    mixed_rows = lax.dot_general(
        rotations[ROTS - 1],
        basis_all,
        (((0,), (0,)), ((), ())),
        preferred_element_type=jnp.float32,
    )
    squares = atoms_sum(jnp.sum(mixed_rows * mixed_rows, axis=1))
    col_norm = jnp.sqrt(squares / total_orbitals + norm_eps)
    return mixed_rows / col_norm[:, None]


def solution(mesh):
    placed = (
        P("bands", "atoms"),
        P("atoms", None),
        P(None, "atoms", None),
        P(None, "atoms", None),
        P(),
        P(None, None, "bands"),
    )
    return jax.shard_map(
        body, mesh=mesh, in_specs=placed, out_specs=P("bands", "atoms"), check_vma=False
    )
```

```python
import jax
import jax.numpy as jnp
from jax import lax
from jax.sharding import PartitionSpec as P

ROUNDS = 2
DEGREE = 8
ROTS = 4
GATHER_AT = 2


filter_center = 0.1
filter_half = 1.25
norm_eps = 1e-06


def swapped(value, axis, stride):
    mask = 2**stride
    pairs = [(source, source ^ mask) for source in range(lax.axis_size(axis))]
    return lax.ppermute(value, axis, pairs)


def gather_bands(value):
    count = lax.axis_size("bands")
    here = lax.axis_index("bands")
    pieces = [value]
    for shift in range(1, count):
        pairs = [(source, (source + shift) % count) for source in range(count)]
        pieces.append(lax.ppermute(value, "bands", pairs))
    order = (here - jnp.arange(count, dtype=jnp.int32)) % count
    return jnp.take(jnp.stack(pieces), order, axis=0)


def gather_pieces(value):
    count = lax.axis_size("bands")
    pieces = [value]
    for shift in range(1, count):
        pairs = [(source, (source + shift) % count) for source in range(count)]
        pieces.append(lax.ppermute(value, "bands", pairs))
    return jnp.stack(pieces)


def atoms_sum(value):
    count = lax.axis_size("atoms")
    stride = 0
    while (1 << stride) < count:
        value = value + swapped(value, "atoms", stride)
        stride += 1
    return value


def atom_index(atom_counts, length_total):
    atom_ends = jnp.cumsum(atom_counts)
    positions = jnp.arange(length_total, dtype=jnp.int32)
    return jnp.sum((positions[:, None] >= atom_ends[None, :]).astype(jnp.int32), axis=1)


def pattern_mask(pattern, row_atoms, col_atoms):
    levels = jnp.arange(pattern.shape[0], dtype=jnp.int32)
    row_onehot = (row_atoms[:, None] == levels[None, :]).astype(jnp.bfloat16)
    per_row = jnp.dot(row_onehot, pattern.astype(jnp.bfloat16), preferred_element_type=jnp.float32)
    mask = jnp.broadcast_to(per_row[:, :1], (row_atoms.shape[0], col_atoms.shape[0]))
    for atom in range(1, pattern.shape[1]):
        mask = jnp.where((col_atoms == atom)[None, :], per_row[:, atom : atom + 1], mask)
    return mask > 0.5


def body(subspace, diag_block, pair_block, pair_pattern, atom_sizes, rotations):
    orb_dev = diag_block.shape[1]
    atoms_dev = pair_pattern.shape[2]
    atoms_here = lax.axis_index("atoms")
    own_atoms = atom_index(
        lax.dynamic_index_in_dim(atom_sizes, atoms_here, 0, keepdims=False), orb_dev
    )
    upper_flag = (own_atoms[:, None] < own_atoms[None, :]).astype(jnp.float32)
    same_atom = (own_atoms[:, None] == own_atoms[None, :]).astype(jnp.float32)
    upper_part = diag_block.astype(jnp.float32) * (upper_flag + 0.5 * same_atom)
    diag_sym = (upper_part + upper_part.T).astype(jnp.bfloat16)
    own_pair_t = []
    other_pair = []
    for round_index in range(ROUNDS):
        partner = jnp.bitwise_xor(atoms_here, 1 << round_index)
        other_atoms = atom_index(
            lax.dynamic_index_in_dim(atom_sizes, partner, 0, keepdims=False), orb_dev
        )
        own_mask = pattern_mask(pair_pattern[round_index], own_atoms, other_atoms)
        own_pair = jnp.where(own_mask, pair_block[round_index], jnp.zeros((), jnp.bfloat16))
        own_pair_t.append(own_pair)
        other_pair.append(swapped(own_pair, "atoms", round_index))

    def apply_operator(values):
        result = jnp.dot(values, diag_sym, preferred_element_type=jnp.float32)
        for round_index in range(ROUNDS):
            other_rows = swapped(values, "atoms", round_index)
            result = result + lax.dot_general(
                other_rows, own_pair_t[round_index], (((1,), (1,)), ((), ())),
                preferred_element_type=jnp.float32,
            )
            result = result + jnp.dot(
                other_rows, other_pair[round_index], preferred_element_type=jnp.float32
            )
        return result

    def chebyshev(start_rows, hook):
        previous = start_rows.astype(jnp.float32)
        current = (apply_operator(start_rows) - filter_center * previous) / filter_half
        for degree_index in range(1, DEGREE):
            if degree_index == GATHER_AT:
                current = hook(current)
            applied = apply_operator(current.astype(jnp.bfloat16))
            following = 2.0 * (applied - filter_center * current) / filter_half - previous
            previous, current = (current, following)
        return current

    gathered = []

    def start_rotation_gather(current):
        held, current = lax.optimization_barrier((rotations[: ROTS - 1], current))
        gathered.append(gather_pieces(held))
        return current

    half_bands = subspace.shape[0] // 2
    current = jnp.concatenate(
        [
            chebyshev(subspace[:half_bands], start_rotation_gather),
            chebyshev(subspace[half_bands:], lambda rows: rows),
        ],
        axis=0,
    )
    rot_pieces = gathered[0]
    total_orbitals = orb_dev * lax.axis_size("atoms")
    band_count = lax.axis_size("bands")
    band_here = lax.axis_index("bands")
    all_bands = rotations.shape[1]
    basis_all = gather_bands(current.astype(jnp.bfloat16)).reshape(all_bands, orb_dev)
    for rotation_index in range(ROTS - 1):
        groups = []
        for group in range(band_count):
            piece = lax.dynamic_index_in_dim(
                rot_pieces, (band_here - group) % band_count, 0, keepdims=False
            )
            groups.append(
                lax.dot_general(
                    piece[rotation_index],
                    basis_all,
                    (((0,), (0,)), ((), ())),
                    preferred_element_type=jnp.float32,
                )
            )
        mixed_rows = jnp.concatenate(groups, axis=0)
        squares = atoms_sum(jnp.sum(mixed_rows * mixed_rows, axis=1))
        col_norm = jnp.sqrt(squares / total_orbitals + norm_eps)
        basis_all = (mixed_rows / col_norm[:, None]).astype(jnp.bfloat16)
    mixed_rows = lax.dot_general(
        rotations[ROTS - 1],
        basis_all,
        (((0,), (0,)), ((), ())),
        preferred_element_type=jnp.float32,
    )
    squares = atoms_sum(jnp.sum(mixed_rows * mixed_rows, axis=1))
    col_norm = jnp.sqrt(squares / total_orbitals + norm_eps)
    return mixed_rows / col_norm[:, None]


def solution(mesh):
    placed = (
        P("bands", "atoms"),
        P("atoms", None),
        P(None, "atoms", None),
        P(None, "atoms", None),
        P(),
        P(None, None, "bands"),
    )
    return jax.shard_map(
        body, mesh=mesh, in_specs=placed, out_specs=P("bands", "atoms"), check_vma=False
    )
```

```python
import jax
import jax.numpy as jnp
from jax import lax
from jax.sharding import PartitionSpec as P

ROUNDS = 2
DEGREE = 8
ROTS = 4
GATHER_AT = 2


filter_center = 0.1
filter_half = 1.25
norm_eps = 1e-06


def swapped(value, axis, stride):
    mask = 2**stride
    pairs = [(source, source ^ mask) for source in range(lax.axis_size(axis))]
    return lax.ppermute(value, axis, pairs)


def gather_bands(value):
    count = lax.axis_size("bands")
    here = lax.axis_index("bands")
    pieces = [value]
    for shift in range(1, count):
        pairs = [(source, (source + shift) % count) for source in range(count)]
        pieces.append(lax.ppermute(value, "bands", pairs))
    order = (here - jnp.arange(count, dtype=jnp.int32)) % count
    return jnp.take(jnp.stack(pieces), order, axis=0)


def gather_pieces(value):
    count = lax.axis_size("bands")
    pieces = [value]
    for shift in range(1, count):
        pairs = [(source, (source + shift) % count) for source in range(count)]
        pieces.append(lax.ppermute(value, "bands", pairs))
    return jnp.stack(pieces)


def atoms_sum(value):
    count = lax.axis_size("atoms")
    stride = 0
    while (1 << stride) < count:
        value = value + swapped(value, "atoms", stride)
        stride += 1
    return value


def atom_index(atom_counts, length_total):
    atom_ends = jnp.cumsum(atom_counts)
    positions = jnp.arange(length_total, dtype=jnp.int32)
    return jnp.sum((positions[:, None] >= atom_ends[None, :]).astype(jnp.int32), axis=1)


def pattern_mask(pattern, row_atoms, col_atoms):
    levels = jnp.arange(pattern.shape[0], dtype=jnp.int32)
    row_onehot = (row_atoms[:, None] == levels[None, :]).astype(jnp.bfloat16)
    col_onehot = (col_atoms[:, None] == levels[None, :]).astype(jnp.bfloat16)
    per_row = jnp.dot(row_onehot, pattern.astype(jnp.bfloat16), preferred_element_type=jnp.float32)
    mask = lax.dot_general(
        per_row.astype(jnp.bfloat16), col_onehot, (((1,), (1,)), ((), ())),
        preferred_element_type=jnp.float32,
    )
    return mask > 0.5


def body(subspace, diag_block, pair_block, pair_pattern, atom_sizes, rotations):
    orb_dev = diag_block.shape[1]
    atoms_dev = pair_pattern.shape[2]
    atoms_here = lax.axis_index("atoms")
    shipped = [swapped(pair_block[r], "atoms", r) for r in range(ROUNDS)]
    shipped_pattern = [swapped(pair_pattern[r], "atoms", r) for r in range(ROUNDS)]
    own_atoms = atom_index(
        lax.dynamic_index_in_dim(atom_sizes, atoms_here, 0, keepdims=False), orb_dev
    )
    upper_flag = (own_atoms[:, None] < own_atoms[None, :]).astype(jnp.float32)
    same_atom = (own_atoms[:, None] == own_atoms[None, :]).astype(jnp.float32)
    upper_part = diag_block.astype(jnp.float32) * (upper_flag + 0.5 * same_atom)
    diag_sym = (upper_part + upper_part.T).astype(jnp.bfloat16)
    own_pair_t = []
    other_pair = []
    for round_index in range(ROUNDS):
        partner = jnp.bitwise_xor(atoms_here, 1 << round_index)
        other_atoms = atom_index(
            lax.dynamic_index_in_dim(atom_sizes, partner, 0, keepdims=False), orb_dev
        )
        own_mask = pattern_mask(pair_pattern[round_index], own_atoms, other_atoms)
        own_pair = jnp.where(own_mask, pair_block[round_index], jnp.zeros((), jnp.bfloat16))
        own_pair_t.append(own_pair)
        other_mask = pattern_mask(shipped_pattern[round_index], other_atoms, own_atoms)
        other_pair.append(
            jnp.where(other_mask, shipped[round_index], jnp.zeros((), jnp.bfloat16))
        )

    def apply_operator(values):
        result = jnp.dot(values, diag_sym, preferred_element_type=jnp.float32)
        for round_index in range(ROUNDS):
            other_rows = swapped(values, "atoms", round_index)
            result = result + lax.dot_general(
                other_rows, own_pair_t[round_index], (((1,), (1,)), ((), ())),
                preferred_element_type=jnp.float32,
            )
            result = result + jnp.dot(
                other_rows, other_pair[round_index], preferred_element_type=jnp.float32
            )
        return result

    def chebyshev(start_rows, hook):
        previous = start_rows.astype(jnp.float32)
        current = (apply_operator(start_rows) - filter_center * previous) / filter_half
        for degree_index in range(1, DEGREE):
            if degree_index == GATHER_AT:
                current = hook(current)
            applied = apply_operator(current.astype(jnp.bfloat16))
            following = 2.0 * (applied - filter_center * current) / filter_half - previous
            previous, current = (current, following)
        return current

    gathered = []

    def start_rotation_gather(current):
        held, current = lax.optimization_barrier((rotations[: ROTS - 1], current))
        half_rows = held.shape[1] // 2
        first_of_pair = (atoms_here % 2) == 0
        mine = jnp.where(first_of_pair, held[:, :half_rows], held[:, half_rows:])
        mine = gather_pieces(mine)
        theirs = swapped(mine, "atoms", 0)
        gathered.append(
            jnp.where(
                first_of_pair,
                jnp.concatenate([mine, theirs], axis=2),
                jnp.concatenate([theirs, mine], axis=2),
            )
        )
        return current

    half_bands = subspace.shape[0] // 2
    current = jnp.concatenate(
        [
            chebyshev(subspace[:half_bands], start_rotation_gather),
            chebyshev(subspace[half_bands:], lambda rows: rows),
        ],
        axis=0,
    )
    rot_pieces = gathered[0]
    total_orbitals = orb_dev * lax.axis_size("atoms")
    band_count = lax.axis_size("bands")
    band_here = lax.axis_index("bands")
    all_bands = rotations.shape[1]
    basis_all = gather_bands(current.astype(jnp.bfloat16)).reshape(all_bands, orb_dev)
    for rotation_index in range(ROTS - 1):
        groups = []
        for group in range(band_count):
            piece = lax.dynamic_index_in_dim(
                rot_pieces, (band_here - group) % band_count, 0, keepdims=False
            )
            groups.append(
                lax.dot_general(
                    piece[rotation_index],
                    basis_all,
                    (((0,), (0,)), ((), ())),
                    preferred_element_type=jnp.float32,
                )
            )
        mixed_rows = jnp.concatenate(groups, axis=0)
        squares = atoms_sum(jnp.sum(mixed_rows * mixed_rows, axis=1))
        col_norm = jnp.sqrt(squares / total_orbitals + norm_eps)
        basis_all = (mixed_rows / col_norm[:, None]).astype(jnp.bfloat16)
    mixed_rows = lax.dot_general(
        rotations[ROTS - 1],
        basis_all,
        (((0,), (0,)), ((), ())),
        preferred_element_type=jnp.float32,
    )
    squares = atoms_sum(jnp.sum(mixed_rows * mixed_rows, axis=1))
    col_norm = jnp.sqrt(squares / total_orbitals + norm_eps)
    return mixed_rows / col_norm[:, None]


def solution(mesh):
    placed = (
        P("bands", "atoms"),
        P("atoms", None),
        P(None, "atoms", None),
        P(None, "atoms", None),
        P(),
        P(None, None, "bands"),
    )
    return jax.shard_map(
        body, mesh=mesh, in_specs=placed, out_specs=P("bands", "atoms"), check_vma=False
    )
```

```python
import jax
import jax.numpy as jnp
from jax import lax
from jax.sharding import PartitionSpec as P

ROUNDS = 2
DEGREE = 8
ROTS = 4
GATHER_AT = 2


filter_center = 0.1
filter_half = 1.25
norm_eps = 1e-06


def swapped(value, axis, stride):
    mask = 2**stride
    pairs = [(source, source ^ mask) for source in range(lax.axis_size(axis))]
    return lax.ppermute(value, axis, pairs)


def gather_bands(value):
    count = lax.axis_size("bands")
    here = lax.axis_index("bands")
    pieces = [value]
    for shift in range(1, count):
        pairs = [(source, (source + shift) % count) for source in range(count)]
        pieces.append(lax.ppermute(value, "bands", pairs))
    order = (here - jnp.arange(count, dtype=jnp.int32)) % count
    return jnp.take(jnp.stack(pieces), order, axis=0)


def gather_pieces(value):
    count = lax.axis_size("bands")
    pieces = [value]
    for shift in range(1, count):
        pairs = [(source, (source + shift) % count) for source in range(count)]
        pieces.append(lax.ppermute(value, "bands", pairs))
    return jnp.stack(pieces)


def atoms_sum(value):
    count = lax.axis_size("atoms")
    stride = 0
    while (1 << stride) < count:
        value = value + swapped(value, "atoms", stride)
        stride += 1
    return value


def atom_index(atom_counts, length_total):
    atom_ends = jnp.cumsum(atom_counts)
    positions = jnp.arange(length_total, dtype=jnp.int32)
    return jnp.sum((positions[:, None] >= atom_ends[None, :]).astype(jnp.int32), axis=1)


def pattern_mask(pattern, row_atoms, col_atoms):
    levels = jnp.arange(pattern.shape[0], dtype=jnp.int32)
    row_onehot = (row_atoms[:, None] == levels[None, :]).astype(jnp.bfloat16)
    col_onehot = (col_atoms[:, None] == levels[None, :]).astype(jnp.bfloat16)
    per_row = jnp.dot(row_onehot, pattern.astype(jnp.bfloat16), preferred_element_type=jnp.float32)
    mask = lax.dot_general(
        per_row.astype(jnp.bfloat16), col_onehot, (((1,), (1,)), ((), ())),
        preferred_element_type=jnp.float32,
    )
    return mask > 0.5


def body(subspace, diag_block, pair_block, pair_pattern, atom_sizes, rotations):
    orb_dev = diag_block.shape[1]
    atoms_dev = pair_pattern.shape[2]
    atoms_here = lax.axis_index("atoms")
    shipped = [swapped(pair_block[r], "atoms", r) for r in range(ROUNDS)]
    shipped_pattern = [swapped(pair_pattern[r], "atoms", r) for r in range(ROUNDS)]
    own_atoms = atom_index(
        lax.dynamic_index_in_dim(atom_sizes, atoms_here, 0, keepdims=False), orb_dev
    )
    upper_flag = (own_atoms[:, None] < own_atoms[None, :]).astype(jnp.float32)
    same_atom = (own_atoms[:, None] == own_atoms[None, :]).astype(jnp.float32)
    upper_part = diag_block.astype(jnp.float32) * (upper_flag + 0.5 * same_atom)
    diag_sym = (upper_part + upper_part.T).astype(jnp.bfloat16)
    own_pair_t = []
    other_pair = []
    for round_index in range(ROUNDS):
        partner = jnp.bitwise_xor(atoms_here, 1 << round_index)
        other_atoms = atom_index(
            lax.dynamic_index_in_dim(atom_sizes, partner, 0, keepdims=False), orb_dev
        )
        own_mask = pattern_mask(pair_pattern[round_index], own_atoms, other_atoms)
        own_pair = jnp.where(own_mask, pair_block[round_index], jnp.zeros((), jnp.bfloat16))
        own_pair_t.append(own_pair)
        other_mask = pattern_mask(shipped_pattern[round_index], other_atoms, own_atoms)
        other_block = jnp.where(other_mask, shipped[round_index], jnp.zeros((), jnp.bfloat16))
        other_pair.append(
            (other_block.astype(jnp.float32) + own_pair.T.astype(jnp.float32)).astype(jnp.bfloat16)
        )

    def apply_operator(values):
        result = jnp.dot(values, diag_sym, preferred_element_type=jnp.float32)
        for round_index in range(ROUNDS):
            other_rows = swapped(values, "atoms", round_index)
            result = result + jnp.dot(
                other_rows, other_pair[round_index], preferred_element_type=jnp.float32
            )
        return result

    def chebyshev(start_rows, hook):
        previous = start_rows.astype(jnp.float32)
        current = (apply_operator(start_rows) - filter_center * previous) / filter_half
        for degree_index in range(1, DEGREE):
            if degree_index == GATHER_AT:
                current = hook(current)
            applied = apply_operator(current.astype(jnp.bfloat16))
            following = 2.0 * (applied - filter_center * current) / filter_half - previous
            previous, current = (current, following)
        return current

    gathered = []

    def start_rotation_gather(current):
        held, current = lax.optimization_barrier((rotations[: ROTS - 1], current))
        half_rows = held.shape[1] // 2
        first_of_pair = (atoms_here % 2) == 0
        mine = jnp.where(first_of_pair, held[:, :half_rows], held[:, half_rows:])
        mine = gather_pieces(mine)
        theirs = swapped(mine, "atoms", 0)
        gathered.append(
            jnp.where(
                first_of_pair,
                jnp.concatenate([mine, theirs], axis=2),
                jnp.concatenate([theirs, mine], axis=2),
            )
        )
        return current

    half_bands = subspace.shape[0] // 2
    current = jnp.concatenate(
        [
            chebyshev(subspace[:half_bands], start_rotation_gather),
            chebyshev(subspace[half_bands:], lambda rows: rows),
        ],
        axis=0,
    )
    rot_pieces = gathered[0]
    total_orbitals = orb_dev * lax.axis_size("atoms")
    band_count = lax.axis_size("bands")
    band_here = lax.axis_index("bands")
    all_bands = rotations.shape[1]
    basis_all = gather_bands(current.astype(jnp.bfloat16)).reshape(all_bands, orb_dev)
    for rotation_index in range(ROTS - 1):
        groups = []
        for group in range(band_count):
            piece = lax.dynamic_index_in_dim(
                rot_pieces, (band_here - group) % band_count, 0, keepdims=False
            )
            groups.append(
                lax.dot_general(
                    piece[rotation_index],
                    basis_all,
                    (((0,), (0,)), ((), ())),
                    preferred_element_type=jnp.float32,
                )
            )
        mixed_rows = jnp.concatenate(groups, axis=0)
        squares = atoms_sum(jnp.sum(mixed_rows * mixed_rows, axis=1))
        col_norm = jnp.sqrt(squares / total_orbitals + norm_eps)
        basis_all = (mixed_rows / col_norm[:, None]).astype(jnp.bfloat16)
    mixed_rows = lax.dot_general(
        rotations[ROTS - 1],
        basis_all,
        (((0,), (0,)), ((), ())),
        preferred_element_type=jnp.float32,
    )
    squares = atoms_sum(jnp.sum(mixed_rows * mixed_rows, axis=1))
    col_norm = jnp.sqrt(squares / total_orbitals + norm_eps)
    return mixed_rows / col_norm[:, None]


def solution(mesh):
    placed = (
        P("bands", "atoms"),
        P("atoms", None),
        P(None, "atoms", None),
        P(None, "atoms", None),
        P(),
        P(None, None, "bands"),
    )
    return jax.shard_map(
        body, mesh=mesh, in_specs=placed, out_specs=P("bands", "atoms"), check_vma=False
    )
```

```python
import jax
import jax.numpy as jnp
from jax import lax
from jax.sharding import PartitionSpec as P

ROUNDS = 2
DEGREE = 8
ROTS = 4
GATHER_AT = 2


filter_center = 0.1
filter_half = 1.25
norm_eps = 1e-06


def swapped(value, axis, stride):
    mask = 2**stride
    pairs = [(source, source ^ mask) for source in range(lax.axis_size(axis))]
    return lax.ppermute(value, axis, pairs)


def gather_bands(value):
    count = lax.axis_size("bands")
    here = lax.axis_index("bands")
    pieces = [value]
    for shift in range(1, count):
        pairs = [(source, (source + shift) % count) for source in range(count)]
        pieces.append(lax.ppermute(value, "bands", pairs))
    order = (here - jnp.arange(count, dtype=jnp.int32)) % count
    return jnp.take(jnp.stack(pieces), order, axis=0)


def gather_pieces(value):
    count = lax.axis_size("bands")
    pieces = [value]
    for shift in range(1, count):
        pairs = [(source, (source + shift) % count) for source in range(count)]
        pieces.append(lax.ppermute(value, "bands", pairs))
    return jnp.stack(pieces)


def atoms_sum(value):
    count = lax.axis_size("atoms")
    stride = 0
    while (1 << stride) < count:
        value = value + swapped(value, "atoms", stride)
        stride += 1
    return value


def atom_index(atom_counts, length_total):
    atom_ends = jnp.cumsum(atom_counts)
    positions = jnp.arange(length_total, dtype=jnp.int32)
    return jnp.sum((positions[:, None] >= atom_ends[None, :]).astype(jnp.int32), axis=1)


def pattern_mask(pattern, row_atoms, col_atoms):
    levels = jnp.arange(pattern.shape[0], dtype=jnp.int32)
    row_onehot = (row_atoms[:, None] == levels[None, :]).astype(jnp.bfloat16)
    col_onehot = (col_atoms[:, None] == levels[None, :]).astype(jnp.bfloat16)
    per_row = jnp.dot(row_onehot, pattern.astype(jnp.bfloat16), preferred_element_type=jnp.float32)
    mask = lax.dot_general(
        per_row.astype(jnp.bfloat16), col_onehot, (((1,), (1,)), ((), ())),
        preferred_element_type=jnp.float32,
    )
    return mask > 0.5


def body(subspace, diag_block, pair_block, pair_pattern, atom_sizes, rotations):
    orb_dev = diag_block.shape[1]
    atoms_dev = pair_pattern.shape[2]
    atoms_here = lax.axis_index("atoms")
    shipped = [swapped(pair_block[r], "atoms", r) for r in range(ROUNDS)]
    shipped_pattern = [swapped(pair_pattern[r], "atoms", r) for r in range(ROUNDS)]
    own_atoms = atom_index(
        lax.dynamic_index_in_dim(atom_sizes, atoms_here, 0, keepdims=False), orb_dev
    )
    row_atom = own_atoms[:, None]
    col_atom = own_atoms[None, :]
    same_atom = 0.5 * (row_atom == col_atom).astype(jnp.float32)
    weight = (row_atom < col_atom).astype(jnp.float32) + same_atom
    weight_t = (col_atom < row_atom).astype(jnp.float32) + same_atom
    diag_sym = (
        diag_block.astype(jnp.float32) * weight + diag_block.T.astype(jnp.float32) * weight_t
    ).astype(jnp.bfloat16)
    other_pair = []
    for round_index in range(ROUNDS):
        partner = jnp.bitwise_xor(atoms_here, 1 << round_index)
        other_atoms = atom_index(
            lax.dynamic_index_in_dim(atom_sizes, partner, 0, keepdims=False), orb_dev
        )
        own_mask_t = pattern_mask(pair_pattern[round_index].T, other_atoms, own_atoms)
        own_block_t = jnp.where(own_mask_t, pair_block[round_index].T, jnp.zeros((), jnp.bfloat16))
        other_mask = pattern_mask(shipped_pattern[round_index], other_atoms, own_atoms)
        other_block = jnp.where(other_mask, shipped[round_index], jnp.zeros((), jnp.bfloat16))
        other_pair.append(
            (other_block.astype(jnp.float32) + own_block_t.astype(jnp.float32)).astype(jnp.bfloat16)
        )

    def apply_operator(values):
        result = jnp.dot(values, diag_sym, preferred_element_type=jnp.float32)
        for round_index in range(ROUNDS):
            other_rows = swapped(values, "atoms", round_index)
            result = result + jnp.dot(
                other_rows, other_pair[round_index], preferred_element_type=jnp.float32
            )
        return result

    def chebyshev(start_rows, hook):
        previous = start_rows.astype(jnp.float32)
        current = (apply_operator(start_rows) - filter_center * previous) / filter_half
        for degree_index in range(1, DEGREE):
            if degree_index == GATHER_AT:
                current = hook(current)
            applied = apply_operator(current.astype(jnp.bfloat16))
            following = 2.0 * (applied - filter_center * current) / filter_half - previous
            previous, current = (current, following)
        return current

    gathered = []

    def start_rotation_gather(current):
        held, current = lax.optimization_barrier((rotations[: ROTS - 1], current))
        gathered.append(gather_pieces(held))
        return current

    half_bands = subspace.shape[0] // 2
    current = jnp.concatenate(
        [
            chebyshev(subspace[:half_bands], start_rotation_gather),
            chebyshev(subspace[half_bands:], lambda rows: rows),
        ],
        axis=0,
    )
    rot_pieces = gathered[0]
    total_orbitals = orb_dev * lax.axis_size("atoms")
    band_count = lax.axis_size("bands")
    band_here = lax.axis_index("bands")
    all_bands = rotations.shape[1]
    basis_all = gather_bands(current.astype(jnp.bfloat16)).reshape(all_bands, orb_dev)
    for rotation_index in range(ROTS - 1):
        groups = []
        for group in range(band_count):
            piece = lax.dynamic_index_in_dim(
                rot_pieces, (band_here - group) % band_count, 0, keepdims=False
            )
            groups.append(
                lax.dot_general(
                    piece[rotation_index],
                    basis_all,
                    (((0,), (0,)), ((), ())),
                    preferred_element_type=jnp.float32,
                )
            )
        mixed_rows = jnp.concatenate(groups, axis=0)
        squares = atoms_sum(jnp.sum(mixed_rows * mixed_rows, axis=1))
        col_norm = jnp.sqrt(squares / total_orbitals + norm_eps)
        basis_all = (mixed_rows / col_norm[:, None]).astype(jnp.bfloat16)
    mixed_rows = lax.dot_general(
        rotations[ROTS - 1],
        basis_all,
        (((0,), (0,)), ((), ())),
        preferred_element_type=jnp.float32,
    )
    squares = atoms_sum(jnp.sum(mixed_rows * mixed_rows, axis=1))
    col_norm = jnp.sqrt(squares / total_orbitals + norm_eps)
    return mixed_rows / col_norm[:, None]


def solution(mesh):
    placed = (
        P("bands", "atoms"),
        P("atoms", None),
        P(None, "atoms", None),
        P(None, "atoms", None),
        P(),
        P(None, None, "bands"),
    )
    return jax.shard_map(
        body, mesh=mesh, in_specs=placed, out_specs=P("bands", "atoms"), check_vma=False
    )
```

```python
import jax
import jax.numpy as jnp
from jax import lax
from jax.sharding import PartitionSpec as P

ROUNDS = 2
DEGREE = 8
ROTS = 4
GATHER_AT = 2


filter_center = 0.1
filter_half = 1.25
norm_eps = 1e-06


def swapped(value, axis, stride):
    mask = 2**stride
    pairs = [(source, source ^ mask) for source in range(lax.axis_size(axis))]
    return lax.ppermute(value, axis, pairs)


def gather_bands(value):
    count = lax.axis_size("bands")
    here = lax.axis_index("bands")
    pieces = [value]
    for shift in range(1, count):
        pairs = [(source, (source + shift) % count) for source in range(count)]
        pieces.append(lax.ppermute(value, "bands", pairs))
    order = (here - jnp.arange(count, dtype=jnp.int32)) % count
    return jnp.take(jnp.stack(pieces), order, axis=0)


def gather_pieces(value):
    count = lax.axis_size("bands")
    pieces = [value]
    for shift in range(1, count):
        pairs = [(source, (source + shift) % count) for source in range(count)]
        pieces.append(lax.ppermute(value, "bands", pairs))
    return jnp.stack(pieces)


def atoms_sum(value):
    count = lax.axis_size("atoms")
    stride = 0
    while (1 << stride) < count:
        value = value + swapped(value, "atoms", stride)
        stride += 1
    return value


def atom_index(atom_counts, length_total):
    atom_ends = jnp.cumsum(atom_counts)
    positions = jnp.arange(length_total, dtype=jnp.int32)
    return jnp.sum((positions[:, None] >= atom_ends[None, :]).astype(jnp.int32), axis=1)


def pattern_mask(pattern, row_atoms, col_atoms):
    levels = jnp.arange(pattern.shape[0], dtype=jnp.int32)
    row_onehot = (row_atoms[:, None] == levels[None, :]).astype(jnp.bfloat16)
    col_onehot = (col_atoms[:, None] == levels[None, :]).astype(jnp.bfloat16)
    per_row = jnp.dot(row_onehot, pattern.astype(jnp.bfloat16), preferred_element_type=jnp.float32)
    mask = lax.dot_general(
        per_row.astype(jnp.bfloat16), col_onehot, (((1,), (1,)), ((), ())),
        preferred_element_type=jnp.float32,
    )
    return mask > 0.5


def body(subspace, diag_block, pair_block, pair_pattern, atom_sizes, rotations):
    orb_dev = diag_block.shape[1]
    atoms_dev = pair_pattern.shape[2]
    atoms_here = lax.axis_index("atoms")
    shipped = [swapped(pair_block[r], "atoms", r) for r in range(ROUNDS)]
    shipped_pattern = [swapped(pair_pattern[r], "atoms", r) for r in range(ROUNDS)]
    own_atoms = atom_index(
        lax.dynamic_index_in_dim(atom_sizes, atoms_here, 0, keepdims=False), orb_dev
    )
    row_atom = own_atoms[:, None]
    col_atom = own_atoms[None, :]
    same_atom = 0.5 * (row_atom == col_atom).astype(jnp.float32)
    weight = (row_atom < col_atom).astype(jnp.float32) + same_atom
    weight_t = (col_atom < row_atom).astype(jnp.float32) + same_atom
    diag_sym = (
        diag_block.astype(jnp.float32) * weight + diag_block.T.astype(jnp.float32) * weight_t
    ).astype(jnp.bfloat16)
    other_pair = []
    for round_index in range(ROUNDS):
        partner = jnp.bitwise_xor(atoms_here, 1 << round_index)
        other_atoms = atom_index(
            lax.dynamic_index_in_dim(atom_sizes, partner, 0, keepdims=False), orb_dev
        )
        own_mask_t = pattern_mask(pair_pattern[round_index].T, other_atoms, own_atoms)
        own_block_t = jnp.where(own_mask_t, pair_block[round_index].T, jnp.zeros((), jnp.bfloat16))
        other_mask = pattern_mask(shipped_pattern[round_index], other_atoms, own_atoms)
        other_block = jnp.where(other_mask, shipped[round_index], jnp.zeros((), jnp.bfloat16))
        other_pair.append(
            (other_block.astype(jnp.float32) + own_block_t.astype(jnp.float32)).astype(jnp.bfloat16)
        )

    def apply_operator(values):
        result = jnp.dot(values, diag_sym, preferred_element_type=jnp.float32)
        for round_index in range(ROUNDS):
            other_rows = swapped(values, "atoms", round_index)
            result = result + jnp.dot(
                other_rows, other_pair[round_index], preferred_element_type=jnp.float32
            )
        return result

    def chebyshev(start_rows, hook):
        previous = start_rows.astype(jnp.float32)
        current = (apply_operator(start_rows) - filter_center * previous) / filter_half
        for degree_index in range(1, DEGREE):
            if degree_index == GATHER_AT:
                current = hook(current)
            applied = apply_operator(current.astype(jnp.bfloat16))
            following = 2.0 * (applied - filter_center * current) / filter_half - previous
            previous, current = (current, following)
        return current

    gathered = []

    def start_rotation_gather(current):
        held, current = lax.optimization_barrier((rotations[: ROTS - 1], current))
        half_rows = held.shape[1] // 2
        first_of_pair = (atoms_here % 2) == 0
        mine = jnp.where(first_of_pair, held[:, :half_rows], held[:, half_rows:])
        mine = gather_pieces(mine)
        gathered.append((mine, swapped(mine, "atoms", 0)))
        return current

    half_bands = subspace.shape[0] // 2
    current = jnp.concatenate(
        [
            chebyshev(subspace[:half_bands], start_rotation_gather),
            chebyshev(subspace[half_bands:], lambda rows: rows),
        ],
        axis=0,
    )
    rot_mine, rot_theirs = gathered[0]
    total_orbitals = orb_dev * lax.axis_size("atoms")
    band_count = lax.axis_size("bands")
    band_here = lax.axis_index("bands")
    all_bands = rotations.shape[1]
    half_rows = all_bands // 2
    mine_start = (atoms_here % 2) * half_rows
    basis_all = gather_bands(current.astype(jnp.bfloat16)).reshape(all_bands, orb_dev)
    for rotation_index in range(ROTS - 1):
        basis_mine = lax.dynamic_slice_in_dim(basis_all, mine_start, half_rows, axis=0)
        basis_theirs = lax.dynamic_slice_in_dim(
            basis_all, half_rows - mine_start, half_rows, axis=0
        )
        groups = []
        for group in range(band_count):
            shift = (band_here - group) % band_count
            piece_mine = lax.dynamic_index_in_dim(rot_mine, shift, 0, keepdims=False)
            piece_theirs = lax.dynamic_index_in_dim(rot_theirs, shift, 0, keepdims=False)
            groups.append(
                lax.dot_general(
                    piece_mine[rotation_index], basis_mine, (((0,), (0,)), ((), ())),
                    preferred_element_type=jnp.float32,
                )
                + lax.dot_general(
                    piece_theirs[rotation_index], basis_theirs, (((0,), (0,)), ((), ())),
                    preferred_element_type=jnp.float32,
                )
            )
        mixed_rows = jnp.concatenate(groups, axis=0)
        squares = atoms_sum(jnp.sum(mixed_rows * mixed_rows, axis=1))
        col_norm = jnp.sqrt(squares / total_orbitals + norm_eps)
        basis_all = (mixed_rows / col_norm[:, None]).astype(jnp.bfloat16)
    mixed_rows = lax.dot_general(
        rotations[ROTS - 1],
        basis_all,
        (((0,), (0,)), ((), ())),
        preferred_element_type=jnp.float32,
    )
    squares = atoms_sum(jnp.sum(mixed_rows * mixed_rows, axis=1))
    col_norm = jnp.sqrt(squares / total_orbitals + norm_eps)
    return mixed_rows / col_norm[:, None]


def solution(mesh):
    placed = (
        P("bands", "atoms"),
        P("atoms", None),
        P(None, "atoms", None),
        P(None, "atoms", None),
        P(),
        P(None, None, "bands"),
    )
    return jax.shard_map(
        body, mesh=mesh, in_specs=placed, out_specs=P("bands", "atoms"), check_vma=False
    )
```

```python
import jax
import jax.numpy as jnp
from jax import lax
from jax.sharding import PartitionSpec as P

ROUNDS = 2
DEGREE = 8
ROTS = 4
GATHER_AT = 2


filter_center = 0.1
filter_half = 1.25
norm_eps = 1e-06


def swapped(value, axis, stride):
    mask = 2**stride
    pairs = [(source, source ^ mask) for source in range(lax.axis_size(axis))]
    return lax.ppermute(value, axis, pairs)


def gather_bands(value):
    count = lax.axis_size("bands")
    here = lax.axis_index("bands")
    pieces = [value]
    for shift in range(1, count):
        pairs = [(source, (source + shift) % count) for source in range(count)]
        pieces.append(lax.ppermute(value, "bands", pairs))
    order = (here - jnp.arange(count, dtype=jnp.int32)) % count
    return jnp.take(jnp.stack(pieces), order, axis=0)


def gather_pieces(value):
    count = lax.axis_size("bands")
    pieces = [value]
    for shift in range(1, count):
        pairs = [(source, (source + shift) % count) for source in range(count)]
        pieces.append(lax.ppermute(value, "bands", pairs))
    return jnp.stack(pieces)


def atoms_sum(value):
    count = lax.axis_size("atoms")
    stride = 0
    while (1 << stride) < count:
        value = value + swapped(value, "atoms", stride)
        stride += 1
    return value


def atom_index(atom_counts, length_total):
    atom_ends = jnp.cumsum(atom_counts)
    positions = jnp.arange(length_total, dtype=jnp.int32)
    return jnp.sum((positions[:, None] >= atom_ends[None, :]).astype(jnp.int32), axis=1)


def pattern_mask(pattern, row_atoms, col_atoms):
    levels = jnp.arange(pattern.shape[0], dtype=jnp.int32)
    row_onehot = (row_atoms[:, None] == levels[None, :]).astype(jnp.bfloat16)
    col_onehot = (col_atoms[:, None] == levels[None, :]).astype(jnp.bfloat16)
    per_row = jnp.dot(row_onehot, pattern.astype(jnp.bfloat16), preferred_element_type=jnp.float32)
    mask = lax.dot_general(
        per_row.astype(jnp.bfloat16), col_onehot, (((1,), (1,)), ((), ())),
        preferred_element_type=jnp.float32,
    )
    return mask > 0.5


def body(subspace, diag_block, pair_block, pair_pattern, atom_sizes, rotations):
    orb_dev = diag_block.shape[1]
    atoms_dev = pair_pattern.shape[2]
    atoms_here = lax.axis_index("atoms")
    shipped = [swapped(pair_block[r], "atoms", r) for r in range(ROUNDS)]
    shipped_pattern = [swapped(pair_pattern[r], "atoms", r) for r in range(ROUNDS)]
    own_atoms = atom_index(
        lax.dynamic_index_in_dim(atom_sizes, atoms_here, 0, keepdims=False), orb_dev
    )
    upper_flag = (own_atoms[:, None] < own_atoms[None, :]).astype(jnp.float32)
    same_atom = (own_atoms[:, None] == own_atoms[None, :]).astype(jnp.float32)
    upper_part = diag_block.astype(jnp.float32) * (upper_flag + 0.5 * same_atom)
    diag_sym = (upper_part + upper_part.T).astype(jnp.bfloat16)
    own_pair_t = []
    other_pair = []
    for round_index in range(ROUNDS):
        partner = jnp.bitwise_xor(atoms_here, 1 << round_index)
        other_atoms = atom_index(
            lax.dynamic_index_in_dim(atom_sizes, partner, 0, keepdims=False), orb_dev
        )
        own_mask = pattern_mask(pair_pattern[round_index], own_atoms, other_atoms)
        own_pair = jnp.where(own_mask, pair_block[round_index], jnp.zeros((), jnp.bfloat16))
        own_pair_t.append(own_pair)
        other_mask = pattern_mask(shipped_pattern[round_index], other_atoms, own_atoms)
        other_block = jnp.where(other_mask, shipped[round_index], jnp.zeros((), jnp.bfloat16))
        other_pair.append(
            (other_block.astype(jnp.float32) + own_pair.T.astype(jnp.float32)).astype(jnp.bfloat16)
        )

    def apply_operator(values):
        result = jnp.dot(values, diag_sym, preferred_element_type=jnp.float32)
        for round_index in range(ROUNDS):
            other_rows = swapped(values, "atoms", round_index)
            result = result + jnp.dot(
                other_rows, other_pair[round_index], preferred_element_type=jnp.float32
            )
        return result

    def chebyshev(start_rows, hook):
        previous = start_rows.astype(jnp.float32)
        current = (apply_operator(start_rows) - filter_center * previous) / filter_half
        for degree_index in range(1, DEGREE):
            if degree_index == GATHER_AT:
                current = hook(current)
            applied = apply_operator(current.astype(jnp.bfloat16))
            following = 2.0 * (applied - filter_center * current) / filter_half - previous
            previous, current = (current, following)
        return current

    gathered = []

    def start_rotation_gather(current):
        held, current = lax.optimization_barrier((rotations[: ROTS - 1], current))
        half_rows = held.shape[1] // 2
        first_of_pair = (atoms_here % 2) == 0
        mine = jnp.where(first_of_pair, held[:, :half_rows], held[:, half_rows:])
        mine = gather_pieces(mine)
        theirs = swapped(mine, "atoms", 0)
        mine_start = (atoms_here % 2) * half_rows
        whole = jnp.zeros(mine.shape[:2] + (2 * half_rows,) + mine.shape[3:], mine.dtype)
        whole = lax.dynamic_update_slice_in_dim(whole, mine, mine_start, axis=2)
        whole = lax.dynamic_update_slice_in_dim(whole, theirs, half_rows - mine_start, axis=2)
        gathered.append(whole)
        return current

    half_bands = subspace.shape[0] // 2
    current = jnp.concatenate(
        [
            chebyshev(subspace[:half_bands], start_rotation_gather),
            chebyshev(subspace[half_bands:], lambda rows: rows),
        ],
        axis=0,
    )
    rot_pieces = gathered[0]
    total_orbitals = orb_dev * lax.axis_size("atoms")
    band_count = lax.axis_size("bands")
    band_here = lax.axis_index("bands")
    all_bands = rotations.shape[1]
    basis_all = gather_bands(current.astype(jnp.bfloat16)).reshape(all_bands, orb_dev)
    for rotation_index in range(ROTS - 1):
        groups = []
        for group in range(band_count):
            piece = lax.dynamic_index_in_dim(
                rot_pieces, (band_here - group) % band_count, 0, keepdims=False
            )
            groups.append(
                lax.dot_general(
                    piece[rotation_index],
                    basis_all,
                    (((0,), (0,)), ((), ())),
                    preferred_element_type=jnp.float32,
                )
            )
        mixed_rows = jnp.concatenate(groups, axis=0)
        squares = atoms_sum(jnp.sum(mixed_rows * mixed_rows, axis=1))
        col_norm = jnp.sqrt(squares / total_orbitals + norm_eps)
        basis_all = (mixed_rows / col_norm[:, None]).astype(jnp.bfloat16)
    mixed_rows = lax.dot_general(
        rotations[ROTS - 1],
        basis_all,
        (((0,), (0,)), ((), ())),
        preferred_element_type=jnp.float32,
    )
    squares = atoms_sum(jnp.sum(mixed_rows * mixed_rows, axis=1))
    col_norm = jnp.sqrt(squares / total_orbitals + norm_eps)
    return mixed_rows / col_norm[:, None]


def solution(mesh):
    placed = (
        P("bands", "atoms"),
        P("atoms", None),
        P(None, "atoms", None),
        P(None, "atoms", None),
        P(),
        P(None, None, "bands"),
    )
    return jax.shard_map(
        body, mesh=mesh, in_specs=placed, out_specs=P("bands", "atoms"), check_vma=False
    )
```

```python
import jax
import jax.numpy as jnp
from jax import lax
from jax.sharding import PartitionSpec as P

ROUNDS = 2
DEGREE = 8
ROTS = 4
GATHER_AT = 0


filter_center = 0.1
filter_half = 1.25
norm_eps = 1e-06


def swapped(value, axis, stride):
    mask = 2**stride
    pairs = [(source, source ^ mask) for source in range(lax.axis_size(axis))]
    return lax.ppermute(value, axis, pairs)


def gather_bands(value):
    count = lax.axis_size("bands")
    here = lax.axis_index("bands")
    pieces = [value]
    for shift in range(1, count):
        pairs = [(source, (source + shift) % count) for source in range(count)]
        pieces.append(lax.ppermute(value, "bands", pairs))
    order = (here - jnp.arange(count, dtype=jnp.int32)) % count
    return jnp.take(jnp.stack(pieces), order, axis=0)


def gather_pieces(value):
    count = lax.axis_size("bands")
    pieces = [value]
    for shift in range(1, count):
        pairs = [(source, (source + shift) % count) for source in range(count)]
        pieces.append(lax.ppermute(value, "bands", pairs))
    return jnp.stack(pieces)


def atoms_sum(value):
    count = lax.axis_size("atoms")
    stride = 0
    while (1 << stride) < count:
        value = value + swapped(value, "atoms", stride)
        stride += 1
    return value


def atom_index(atom_counts, length_total):
    atom_ends = jnp.cumsum(atom_counts)
    positions = jnp.arange(length_total, dtype=jnp.int32)
    return jnp.sum((positions[:, None] >= atom_ends[None, :]).astype(jnp.int32), axis=1)


def pattern_mask(pattern, row_atoms, col_atoms):
    levels = jnp.arange(pattern.shape[0], dtype=jnp.int32)
    row_onehot = (row_atoms[:, None] == levels[None, :]).astype(jnp.bfloat16)
    col_onehot = (col_atoms[:, None] == levels[None, :]).astype(jnp.bfloat16)
    per_row = jnp.dot(row_onehot, pattern.astype(jnp.bfloat16), preferred_element_type=jnp.float32)
    mask = lax.dot_general(
        per_row.astype(jnp.bfloat16), col_onehot, (((1,), (1,)), ((), ())),
        preferred_element_type=jnp.float32,
    )
    return mask > 0.5


def body(subspace, diag_block, pair_block, pair_pattern, atom_sizes, rotations):
    orb_dev = diag_block.shape[1]
    atoms_dev = pair_pattern.shape[2]
    atoms_here = lax.axis_index("atoms")
    shipped = [swapped(pair_block[r], "atoms", r) for r in range(ROUNDS)]
    shipped_pattern = [swapped(pair_pattern[r], "atoms", r) for r in range(ROUNDS)]
    own_atoms = atom_index(
        lax.dynamic_index_in_dim(atom_sizes, atoms_here, 0, keepdims=False), orb_dev
    )
    upper_flag = (own_atoms[:, None] < own_atoms[None, :]).astype(jnp.float32)
    same_atom = (own_atoms[:, None] == own_atoms[None, :]).astype(jnp.float32)
    upper_part = diag_block.astype(jnp.float32) * (upper_flag + 0.5 * same_atom)
    diag_sym = (upper_part + upper_part.T).astype(jnp.bfloat16)
    own_pair_t = []
    other_pair = []
    for round_index in range(ROUNDS):
        partner = jnp.bitwise_xor(atoms_here, 1 << round_index)
        other_atoms = atom_index(
            lax.dynamic_index_in_dim(atom_sizes, partner, 0, keepdims=False), orb_dev
        )
        own_mask = pattern_mask(pair_pattern[round_index], own_atoms, other_atoms)
        own_pair = jnp.where(own_mask, pair_block[round_index], jnp.zeros((), jnp.bfloat16))
        own_pair_t.append(own_pair)
        other_mask = pattern_mask(shipped_pattern[round_index], other_atoms, own_atoms)
        other_block = jnp.where(other_mask, shipped[round_index], jnp.zeros((), jnp.bfloat16))
        other_pair.append(
            (other_block.astype(jnp.float32) + own_pair.T.astype(jnp.float32)).astype(jnp.bfloat16)
        )

    def apply_operator(values):
        result = jnp.dot(values, diag_sym, preferred_element_type=jnp.float32)
        for round_index in range(ROUNDS):
            other_rows = swapped(values, "atoms", round_index)
            result = result + jnp.dot(
                other_rows, other_pair[round_index], preferred_element_type=jnp.float32
            )
        return result

    def chebyshev(start_rows, hook):
        if GATHER_AT == 0:
            start_rows = hook(start_rows)
        previous = start_rows.astype(jnp.float32)
        current = (apply_operator(start_rows) - filter_center * previous) / filter_half
        for degree_index in range(1, DEGREE):
            if degree_index == GATHER_AT:
                current = hook(current)
            applied = apply_operator(current.astype(jnp.bfloat16))
            following = 2.0 * (applied - filter_center * current) / filter_half - previous
            previous, current = (current, following)
        return current

    gathered = []

    def start_rotation_gather(current):
        held, current = lax.optimization_barrier((rotations[: ROTS - 1], current))
        half_rows = held.shape[1] // 2
        first_of_pair = (atoms_here % 2) == 0
        mine = jnp.where(first_of_pair, held[:, :half_rows], held[:, half_rows:])
        mine = gather_pieces(mine)
        theirs = swapped(mine, "atoms", 0)
        mine_start = (atoms_here % 2) * half_rows
        whole = jnp.zeros(mine.shape[:2] + (2 * half_rows,) + mine.shape[3:], mine.dtype)
        whole = lax.dynamic_update_slice_in_dim(whole, mine, mine_start, axis=2)
        whole = lax.dynamic_update_slice_in_dim(whole, theirs, half_rows - mine_start, axis=2)
        gathered.append(whole)
        return current

    half_bands = subspace.shape[0] // 2
    current = jnp.concatenate(
        [
            chebyshev(subspace[:half_bands], start_rotation_gather),
            chebyshev(subspace[half_bands:], lambda rows: rows),
        ],
        axis=0,
    )
    rot_pieces = gathered[0]
    total_orbitals = orb_dev * lax.axis_size("atoms")
    band_count = lax.axis_size("bands")
    band_here = lax.axis_index("bands")
    all_bands = rotations.shape[1]
    basis_all = gather_bands(current.astype(jnp.bfloat16)).reshape(all_bands, orb_dev)
    for rotation_index in range(ROTS - 1):
        groups = []
        for group in range(band_count):
            piece = lax.dynamic_index_in_dim(
                rot_pieces, (band_here - group) % band_count, 0, keepdims=False
            )
            groups.append(
                lax.dot_general(
                    piece[rotation_index],
                    basis_all,
                    (((0,), (0,)), ((), ())),
                    preferred_element_type=jnp.float32,
                )
            )
        mixed_rows = jnp.concatenate(groups, axis=0)
        squares = atoms_sum(jnp.sum(mixed_rows * mixed_rows, axis=1))
        col_norm = jnp.sqrt(squares / total_orbitals + norm_eps)
        basis_all = (mixed_rows / col_norm[:, None]).astype(jnp.bfloat16)
    mixed_rows = lax.dot_general(
        rotations[ROTS - 1],
        basis_all,
        (((0,), (0,)), ((), ())),
        preferred_element_type=jnp.float32,
    )
    squares = atoms_sum(jnp.sum(mixed_rows * mixed_rows, axis=1))
    col_norm = jnp.sqrt(squares / total_orbitals + norm_eps)
    return mixed_rows / col_norm[:, None]


def solution(mesh):
    placed = (
        P("bands", "atoms"),
        P("atoms", None),
        P(None, "atoms", None),
        P(None, "atoms", None),
        P(),
        P(None, None, "bands"),
    )
    return jax.shard_map(
        body, mesh=mesh, in_specs=placed, out_specs=P("bands", "atoms"), check_vma=False
    )
```

```python
import jax
import jax.numpy as jnp
from jax import lax
from jax.sharding import PartitionSpec as P

ROUNDS = 2
DEGREE = 8
ROTS = 4
GATHER_AT = 2


filter_center = 0.1
filter_half = 1.25
norm_eps = 1e-06


def swapped(value, axis, stride):
    mask = 2**stride
    pairs = [(source, source ^ mask) for source in range(lax.axis_size(axis))]
    return lax.ppermute(value, axis, pairs)


def gather_bands(value):
    count = lax.axis_size("bands")
    here = lax.axis_index("bands")
    pieces = [value]
    for shift in range(1, count):
        pairs = [(source, (source + shift) % count) for source in range(count)]
        pieces.append(lax.ppermute(value, "bands", pairs))
    order = (here - jnp.arange(count, dtype=jnp.int32)) % count
    return jnp.take(jnp.stack(pieces), order, axis=0)


def gather_pieces(value):
    count = lax.axis_size("bands")
    pieces = [value]
    for shift in range(1, count):
        pairs = [(source, (source + shift) % count) for source in range(count)]
        pieces.append(lax.ppermute(value, "bands", pairs))
    return jnp.stack(pieces)


def atoms_sum(value):
    count = lax.axis_size("atoms")
    stride = 0
    while (1 << stride) < count:
        value = value + swapped(value, "atoms", stride)
        stride += 1
    return value


def atom_index(atom_counts, length_total):
    atom_ends = jnp.cumsum(atom_counts)
    positions = jnp.arange(length_total, dtype=jnp.int32)
    return jnp.sum((positions[:, None] >= atom_ends[None, :]).astype(jnp.int32), axis=1)


def pattern_mask(pattern, row_atoms, col_atoms):
    levels = jnp.arange(pattern.shape[0], dtype=jnp.int32)
    row_onehot = (row_atoms[:, None] == levels[None, :]).astype(jnp.bfloat16)
    col_onehot = (col_atoms[:, None] == levels[None, :]).astype(jnp.bfloat16)
    per_row = jnp.dot(row_onehot, pattern.astype(jnp.bfloat16), preferred_element_type=jnp.float32)
    mask = lax.dot_general(
        per_row.astype(jnp.bfloat16), col_onehot, (((1,), (1,)), ((), ())),
        preferred_element_type=jnp.float32,
    )
    return mask > 0.5


def body(subspace, diag_block, pair_block, pair_pattern, atom_sizes, rotations):
    orb_dev = diag_block.shape[1]
    atoms_dev = pair_pattern.shape[2]
    atoms_here = lax.axis_index("atoms")
    shipped = [swapped(pair_block[r], "atoms", r) for r in range(ROUNDS)]
    shipped_pattern = [swapped(pair_pattern[r], "atoms", r) for r in range(ROUNDS)]
    own_atoms = atom_index(
        lax.dynamic_index_in_dim(atom_sizes, atoms_here, 0, keepdims=False), orb_dev
    )
    row_atom = own_atoms[:, None]
    col_atom = own_atoms[None, :]
    same_atom = 0.5 * (row_atom == col_atom).astype(jnp.float32)
    weight = (row_atom < col_atom).astype(jnp.float32) + same_atom
    weight_t = (col_atom < row_atom).astype(jnp.float32) + same_atom
    diag_sym = (
        diag_block.astype(jnp.float32) * weight + diag_block.T.astype(jnp.float32) * weight_t
    ).astype(jnp.bfloat16)
    other_pair = []
    for round_index in range(ROUNDS):
        partner = jnp.bitwise_xor(atoms_here, 1 << round_index)
        other_atoms = atom_index(
            lax.dynamic_index_in_dim(atom_sizes, partner, 0, keepdims=False), orb_dev
        )
        own_mask_t = pattern_mask(pair_pattern[round_index].T, other_atoms, own_atoms)
        own_block_t = jnp.where(own_mask_t, pair_block[round_index].T, jnp.zeros((), jnp.bfloat16))
        other_mask = pattern_mask(shipped_pattern[round_index], other_atoms, own_atoms)
        other_block = jnp.where(other_mask, shipped[round_index], jnp.zeros((), jnp.bfloat16))
        other_pair.append(
            (other_block.astype(jnp.float32) + own_block_t.astype(jnp.float32)).astype(jnp.bfloat16)
        )

    def apply_operator(values):
        result = jnp.dot(values, diag_sym, preferred_element_type=jnp.float32)
        for round_index in range(ROUNDS):
            other_rows = swapped(values, "atoms", round_index)
            result = result + jnp.dot(
                other_rows, other_pair[round_index], preferred_element_type=jnp.float32
            )
        return result

    def chebyshev(start_rows, hook):
        previous = start_rows.astype(jnp.float32)
        current = (apply_operator(start_rows) - filter_center * previous) / filter_half
        for degree_index in range(1, DEGREE):
            if degree_index == GATHER_AT:
                current = hook(current)
            applied = apply_operator(current.astype(jnp.bfloat16))
            following = 2.0 * (applied - filter_center * current) / filter_half - previous
            previous, current = (current, following)
        return current

    gathered = []

    def start_rotation_gather(current):
        held, current = lax.optimization_barrier((rotations, current))
        half_rows = held.shape[1] // 2
        first_of_pair = (atoms_here % 2) == 0
        mine = jnp.where(
            first_of_pair, held[: ROTS - 1, :half_rows], held[: ROTS - 1, half_rows:]
        )
        mine = gather_pieces(mine)
        theirs = swapped(mine, "atoms", 0)
        mine_start = (atoms_here % 2) * half_rows
        whole = jnp.zeros(mine.shape[:2] + (2 * half_rows,) + mine.shape[3:], mine.dtype)
        whole = lax.dynamic_update_slice_in_dim(whole, mine, mine_start, axis=2)
        whole = lax.dynamic_update_slice_in_dim(whole, theirs, half_rows - mine_start, axis=2)
        gathered.append(whole)
        return current

    half_bands = subspace.shape[0] // 2
    current = jnp.concatenate(
        [
            chebyshev(subspace[:half_bands], start_rotation_gather),
            chebyshev(subspace[half_bands:], lambda rows: rows),
        ],
        axis=0,
    )
    rot_pieces = gathered[0]
    total_orbitals = orb_dev * lax.axis_size("atoms")
    band_count = lax.axis_size("bands")
    band_here = lax.axis_index("bands")
    all_bands = rotations.shape[1]
    basis_all = gather_bands(current.astype(jnp.bfloat16)).reshape(all_bands, orb_dev)
    for rotation_index in range(ROTS - 1):
        groups = []
        for group in range(band_count):
            piece = lax.dynamic_index_in_dim(
                rot_pieces, (band_here - group) % band_count, 0, keepdims=False
            )
            groups.append(
                lax.dot_general(
                    piece[rotation_index],
                    basis_all,
                    (((0,), (0,)), ((), ())),
                    preferred_element_type=jnp.float32,
                )
            )
        mixed_rows = jnp.concatenate(groups, axis=0)
        squares = atoms_sum(jnp.sum(mixed_rows * mixed_rows, axis=1))
        col_norm = jnp.sqrt(squares / total_orbitals + norm_eps)
        basis_all = (mixed_rows / col_norm[:, None]).astype(jnp.bfloat16)
    mixed_rows = lax.dot_general(
        rotations[ROTS - 1],
        basis_all,
        (((0,), (0,)), ((), ())),
        preferred_element_type=jnp.float32,
    )
    squares = atoms_sum(jnp.sum(mixed_rows * mixed_rows, axis=1))
    col_norm = jnp.sqrt(squares / total_orbitals + norm_eps)
    return mixed_rows / col_norm[:, None]


def solution(mesh):
    placed = (
        P("bands", "atoms"),
        P("atoms", None),
        P(None, "atoms", None),
        P(None, "atoms", None),
        P(),
        P(None, None, "bands"),
    )
    return jax.shard_map(
        body, mesh=mesh, in_specs=placed, out_specs=P("bands", "atoms"), check_vma=False
    )
```

```python
import jax
import jax.numpy as jnp
from jax import lax
from jax.sharding import PartitionSpec as P

ROUNDS = 2
DEGREE = 8
ROTS = 4
GATHER_AT = 2


filter_center = 0.1
filter_half = 1.25
norm_eps = 1e-06


def swapped(value, axis, stride):
    mask = 2**stride
    pairs = [(source, source ^ mask) for source in range(lax.axis_size(axis))]
    return lax.ppermute(value, axis, pairs)


def gather_bands(value):
    count = lax.axis_size("bands")
    here = lax.axis_index("bands")
    pieces = [value]
    for shift in range(1, count):
        pairs = [(source, (source + shift) % count) for source in range(count)]
        pieces.append(lax.ppermute(value, "bands", pairs))
    order = (here - jnp.arange(count, dtype=jnp.int32)) % count
    return jnp.take(jnp.stack(pieces), order, axis=0)


def gather_pieces(value):
    count = lax.axis_size("bands")
    pieces = [value]
    for shift in range(1, count):
        pairs = [(source, (source + shift) % count) for source in range(count)]
        pieces.append(lax.ppermute(value, "bands", pairs))
    return jnp.stack(pieces)


def atoms_sum(value):
    count = lax.axis_size("atoms")
    stride = 0
    while (1 << stride) < count:
        value = value + swapped(value, "atoms", stride)
        stride += 1
    return value


def atom_index(atom_counts, length_total):
    atom_ends = jnp.cumsum(atom_counts)
    positions = jnp.arange(length_total, dtype=jnp.int32)
    return jnp.sum((positions[:, None] >= atom_ends[None, :]).astype(jnp.int32), axis=1)


def pattern_mask(pattern, row_atoms, col_atoms):
    levels = jnp.arange(pattern.shape[0], dtype=jnp.int32)
    row_onehot = (row_atoms[:, None] == levels[None, :]).astype(jnp.bfloat16)
    col_onehot = (col_atoms[:, None] == levels[None, :]).astype(jnp.bfloat16)
    per_row = jnp.dot(row_onehot, pattern.astype(jnp.bfloat16), preferred_element_type=jnp.float32)
    mask = lax.dot_general(
        per_row.astype(jnp.bfloat16), col_onehot, (((1,), (1,)), ((), ())),
        preferred_element_type=jnp.float32,
    )
    return mask > 0.5


def body(subspace, diag_block, pair_block, pair_pattern, atom_sizes, rotations):
    orb_dev = diag_block.shape[1]
    atoms_dev = pair_pattern.shape[2]
    atoms_here = lax.axis_index("atoms")
    shipped = [swapped(pair_block[r], "atoms", r) for r in range(ROUNDS)]
    shipped_pattern = [swapped(pair_pattern[r], "atoms", r) for r in range(ROUNDS)]
    own_atoms = atom_index(
        lax.dynamic_index_in_dim(atom_sizes, atoms_here, 0, keepdims=False), orb_dev
    )
    row_atom = own_atoms[:, None]
    col_atom = own_atoms[None, :]
    same_atom = 0.5 * (row_atom == col_atom).astype(jnp.float32)
    weight = (row_atom < col_atom).astype(jnp.float32) + same_atom
    weight_t = (col_atom < row_atom).astype(jnp.float32) + same_atom
    diag_sym = (
        diag_block.astype(jnp.float32) * weight + diag_block.T.astype(jnp.float32) * weight_t
    ).astype(jnp.bfloat16)
    other_pair = []
    for round_index in range(ROUNDS):
        partner = jnp.bitwise_xor(atoms_here, 1 << round_index)
        other_atoms = atom_index(
            lax.dynamic_index_in_dim(atom_sizes, partner, 0, keepdims=False), orb_dev
        )
        own_mask_t = pattern_mask(pair_pattern[round_index].T, other_atoms, own_atoms)
        own_block_t = jnp.where(own_mask_t, pair_block[round_index].T, jnp.zeros((), jnp.bfloat16))
        other_mask = pattern_mask(shipped_pattern[round_index], other_atoms, own_atoms)
        other_block = jnp.where(other_mask, shipped[round_index], jnp.zeros((), jnp.bfloat16))
        other_pair.append(
            (other_block.astype(jnp.float32) + own_block_t.astype(jnp.float32)).astype(jnp.bfloat16)
        )

    def apply_operator(values, received=None):
        result = jnp.dot(values, diag_sym, preferred_element_type=jnp.float32)
        for round_index in range(ROUNDS):
            if received is None:
                other_rows = swapped(values, "atoms", round_index)
            else:
                other_rows = received[round_index]
            result = result + jnp.dot(
                other_rows, other_pair[round_index], preferred_element_type=jnp.float32
            )
        return result

    def chebyshev(start_rows, hook, received):
        previous = start_rows.astype(jnp.float32)
        current = (apply_operator(start_rows, received) - filter_center * previous) / filter_half
        for degree_index in range(1, DEGREE):
            if degree_index == GATHER_AT:
                current = hook(current)
            applied = apply_operator(current.astype(jnp.bfloat16))
            following = 2.0 * (applied - filter_center * current) / filter_half - previous
            previous, current = (current, following)
        return current

    gathered = []

    def start_rotation_gather(current):
        held, current = lax.optimization_barrier((rotations, current))
        half_rows = held.shape[1] // 2
        first_of_pair = (atoms_here % 2) == 0
        mine = jnp.where(
            first_of_pair, held[: ROTS - 1, :half_rows], held[: ROTS - 1, half_rows:]
        )
        mine = gather_pieces(mine)
        theirs = swapped(mine, "atoms", 0)
        mine_start = (atoms_here % 2) * half_rows
        whole = jnp.zeros(mine.shape[:2] + (2 * half_rows,) + mine.shape[3:], mine.dtype)
        whole = lax.dynamic_update_slice_in_dim(whole, mine, mine_start, axis=2)
        whole = lax.dynamic_update_slice_in_dim(whole, theirs, half_rows - mine_start, axis=2)
        gathered.append(whole)
        return current

    half_bands = subspace.shape[0] // 2
    first_rows = [swapped(subspace, "atoms", r) for r in range(ROUNDS)]
    current = jnp.concatenate(
        [
            chebyshev(
                subspace[:half_bands], start_rotation_gather,
                [rows[:half_bands] for rows in first_rows],
            ),
            chebyshev(
                subspace[half_bands:], lambda rows: rows,
                [rows[half_bands:] for rows in first_rows],
            ),
        ],
        axis=0,
    )
    rot_pieces = gathered[0]
    total_orbitals = orb_dev * lax.axis_size("atoms")
    band_count = lax.axis_size("bands")
    band_here = lax.axis_index("bands")
    all_bands = rotations.shape[1]
    basis_all = gather_bands(current.astype(jnp.bfloat16)).reshape(all_bands, orb_dev)
    for rotation_index in range(ROTS - 1):
        groups = []
        for group in range(band_count):
            piece = lax.dynamic_index_in_dim(
                rot_pieces, (band_here - group) % band_count, 0, keepdims=False
            )
            groups.append(
                lax.dot_general(
                    piece[rotation_index],
                    basis_all,
                    (((0,), (0,)), ((), ())),
                    preferred_element_type=jnp.float32,
                )
            )
        mixed_rows = jnp.concatenate(groups, axis=0)
        squares = atoms_sum(jnp.sum(mixed_rows * mixed_rows, axis=1))
        col_norm = jnp.sqrt(squares / total_orbitals + norm_eps)
        basis_all = (mixed_rows / col_norm[:, None]).astype(jnp.bfloat16)
    mixed_rows = lax.dot_general(
        rotations[ROTS - 1],
        basis_all,
        (((0,), (0,)), ((), ())),
        preferred_element_type=jnp.float32,
    )
    squares = atoms_sum(jnp.sum(mixed_rows * mixed_rows, axis=1))
    col_norm = jnp.sqrt(squares / total_orbitals + norm_eps)
    return mixed_rows / col_norm[:, None]


def solution(mesh):
    placed = (
        P("bands", "atoms"),
        P("atoms", None),
        P(None, "atoms", None),
        P(None, "atoms", None),
        P(),
        P(None, None, "bands"),
    )
    return jax.shard_map(
        body, mesh=mesh, in_specs=placed, out_specs=P("bands", "atoms"), check_vma=False
    )
```

```python
import jax
import jax.numpy as jnp
from jax import lax
from jax.sharding import PartitionSpec as P

ROUNDS = 2
DEGREE = 8
ROTS = 4
GATHER_AT = 2


filter_center = 0.1
filter_half = 1.25
norm_eps = 1e-06


def swapped(value, axis, stride):
    mask = 2**stride
    pairs = [(source, source ^ mask) for source in range(lax.axis_size(axis))]
    return lax.ppermute(value, axis, pairs)


def gather_bands(value):
    count = lax.axis_size("bands")
    here = lax.axis_index("bands")
    pieces = [value]
    for shift in range(1, count):
        pairs = [(source, (source + shift) % count) for source in range(count)]
        pieces.append(lax.ppermute(value, "bands", pairs))
    order = (here - jnp.arange(count, dtype=jnp.int32)) % count
    return jnp.take(jnp.stack(pieces), order, axis=0)


def gather_pieces(value):
    count = lax.axis_size("bands")
    pieces = [value]
    for shift in range(1, count):
        pairs = [(source, (source + shift) % count) for source in range(count)]
        pieces.append(lax.ppermute(value, "bands", pairs))
    return jnp.stack(pieces)


def atoms_sum(value):
    count = lax.axis_size("atoms")
    stride = 0
    while (1 << stride) < count:
        value = value + swapped(value, "atoms", stride)
        stride += 1
    return value


def atom_index(atom_counts, length_total):
    atom_ends = jnp.cumsum(atom_counts)
    positions = jnp.arange(length_total, dtype=jnp.int32)
    return jnp.sum((positions[:, None] >= atom_ends[None, :]).astype(jnp.int32), axis=1)


def pattern_mask(pattern, row_atoms, col_atoms):
    levels = jnp.arange(pattern.shape[0], dtype=jnp.int32)
    row_onehot = (row_atoms[:, None] == levels[None, :]).astype(jnp.bfloat16)
    col_onehot = (col_atoms[:, None] == levels[None, :]).astype(jnp.bfloat16)
    per_row = jnp.dot(row_onehot, pattern.astype(jnp.bfloat16), preferred_element_type=jnp.float32)
    mask = lax.dot_general(
        per_row.astype(jnp.bfloat16), col_onehot, (((1,), (1,)), ((), ())),
        preferred_element_type=jnp.float32,
    )
    return mask > 0.5


def body(subspace, diag_block, pair_block, pair_pattern, atom_sizes, rotations):
    orb_dev = diag_block.shape[1]
    atoms_dev = pair_pattern.shape[2]
    atoms_here = lax.axis_index("atoms")
    shipped = [swapped(pair_block[r], "atoms", r) for r in range(ROUNDS)]
    shipped_pattern = [swapped(pair_pattern[r], "atoms", r) for r in range(ROUNDS)]
    own_atoms = atom_index(
        lax.dynamic_index_in_dim(atom_sizes, atoms_here, 0, keepdims=False), orb_dev
    )
    row_atom = own_atoms[:, None]
    col_atom = own_atoms[None, :]
    same_atom = 0.5 * (row_atom == col_atom).astype(jnp.float32)
    weight = (row_atom < col_atom).astype(jnp.float32) + same_atom
    weight_t = (col_atom < row_atom).astype(jnp.float32) + same_atom
    diag_sym = (
        diag_block.astype(jnp.float32) * weight + diag_block.T.astype(jnp.float32) * weight_t
    ).astype(jnp.bfloat16)
    other_pair = []
    for round_index in range(ROUNDS):
        partner = jnp.bitwise_xor(atoms_here, 1 << round_index)
        other_atoms = atom_index(
            lax.dynamic_index_in_dim(atom_sizes, partner, 0, keepdims=False), orb_dev
        )
        own_mask_t = pattern_mask(pair_pattern[round_index].T, other_atoms, own_atoms)
        own_block_t = jnp.where(own_mask_t, pair_block[round_index].T, jnp.zeros((), jnp.bfloat16))
        other_mask = pattern_mask(shipped_pattern[round_index], other_atoms, own_atoms)
        other_block = jnp.where(other_mask, shipped[round_index], jnp.zeros((), jnp.bfloat16))
        other_pair.append(
            (other_block.astype(jnp.float32) + own_block_t.astype(jnp.float32)).astype(jnp.bfloat16)
        )

    def apply_operator(values):
        result = jnp.dot(values, diag_sym, preferred_element_type=jnp.float32)
        for round_index in range(ROUNDS):
            other_rows = swapped(values, "atoms", round_index)
            result = result + jnp.dot(
                other_rows, other_pair[round_index], preferred_element_type=jnp.float32
            )
        return result

    def chebyshev(start_rows, hook):
        previous = start_rows.astype(jnp.float32)
        current = (apply_operator(start_rows) - filter_center * previous) / filter_half
        for degree_index in range(1, DEGREE):
            if degree_index == GATHER_AT:
                current = hook(current)
            if degree_index == DEGREE - 1 and gathered:
                settled, current = lax.optimization_barrier((gathered[0], current))
                gathered[0] = settled
            applied = apply_operator(current.astype(jnp.bfloat16))
            following = 2.0 * (applied - filter_center * current) / filter_half - previous
            previous, current = (current, following)
        return current

    gathered = []

    def start_rotation_gather(current):
        held, current = lax.optimization_barrier((rotations, current))
        half_rows = held.shape[1] // 2
        first_of_pair = (atoms_here % 2) == 0
        mine = jnp.where(
            first_of_pair, held[: ROTS - 1, :half_rows], held[: ROTS - 1, half_rows:]
        )
        mine = gather_pieces(mine)
        theirs = swapped(mine, "atoms", 0)
        mine_start = (atoms_here % 2) * half_rows
        whole = jnp.zeros(mine.shape[:2] + (2 * half_rows,) + mine.shape[3:], mine.dtype)
        whole = lax.dynamic_update_slice_in_dim(whole, mine, mine_start, axis=2)
        whole = lax.dynamic_update_slice_in_dim(whole, theirs, half_rows - mine_start, axis=2)
        gathered.append(whole)
        return current

    half_bands = subspace.shape[0] // 2
    current = jnp.concatenate(
        [
            chebyshev(subspace[:half_bands], start_rotation_gather),
            chebyshev(subspace[half_bands:], lambda rows: rows),
        ],
        axis=0,
    )
    rot_pieces = gathered[0]
    total_orbitals = orb_dev * lax.axis_size("atoms")
    band_count = lax.axis_size("bands")
    band_here = lax.axis_index("bands")
    all_bands = rotations.shape[1]
    basis_all = gather_bands(current.astype(jnp.bfloat16)).reshape(all_bands, orb_dev)
    for rotation_index in range(ROTS - 1):
        groups = []
        for group in range(band_count):
            piece = lax.dynamic_index_in_dim(
                rot_pieces, (band_here - group) % band_count, 0, keepdims=False
            )
            groups.append(
                lax.dot_general(
                    piece[rotation_index],
                    basis_all,
                    (((0,), (0,)), ((), ())),
                    preferred_element_type=jnp.float32,
                )
            )
        mixed_rows = jnp.concatenate(groups, axis=0)
        squares = atoms_sum(jnp.sum(mixed_rows * mixed_rows, axis=1))
        col_norm = jnp.sqrt(squares / total_orbitals + norm_eps)
        basis_all = (mixed_rows / col_norm[:, None]).astype(jnp.bfloat16)
    mixed_rows = lax.dot_general(
        rotations[ROTS - 1],
        basis_all,
        (((0,), (0,)), ((), ())),
        preferred_element_type=jnp.float32,
    )
    squares = atoms_sum(jnp.sum(mixed_rows * mixed_rows, axis=1))
    col_norm = jnp.sqrt(squares / total_orbitals + norm_eps)
    return mixed_rows / col_norm[:, None]


def solution(mesh):
    placed = (
        P("bands", "atoms"),
        P("atoms", None),
        P(None, "atoms", None),
        P(None, "atoms", None),
        P(),
        P(None, None, "bands"),
    )
    return jax.shard_map(
        body, mesh=mesh, in_specs=placed, out_specs=P("bands", "atoms"), check_vma=False
    )
```

```python
import jax
import jax.numpy as jnp
from jax import lax
from jax.sharding import PartitionSpec as P

ROUNDS = 2
DEGREE = 8
ROTS = 4
GATHER_AT = 2


filter_center = 0.1
filter_half = 1.25
norm_eps = 1e-06


def swapped(value, axis, stride):
    mask = 2**stride
    pairs = [(source, source ^ mask) for source in range(lax.axis_size(axis))]
    return lax.ppermute(value, axis, pairs)


def gather_bands(value):
    count = lax.axis_size("bands")
    here = lax.axis_index("bands")
    pieces = [value]
    for shift in range(1, count):
        pairs = [(source, (source + shift) % count) for source in range(count)]
        pieces.append(lax.ppermute(value, "bands", pairs))
    order = (here - jnp.arange(count, dtype=jnp.int32)) % count
    return jnp.take(jnp.stack(pieces), order, axis=0)


def gather_pieces(value):
    count = lax.axis_size("bands")
    pieces = [value]
    for shift in range(1, count):
        pairs = [(source, (source + shift) % count) for source in range(count)]
        pieces.append(lax.ppermute(value, "bands", pairs))
    return jnp.stack(pieces)


def atoms_sum(value):
    count = lax.axis_size("atoms")
    stride = 0
    while (1 << stride) < count:
        value = value + swapped(value, "atoms", stride)
        stride += 1
    return value


def atom_index(atom_counts, length_total):
    atom_ends = jnp.cumsum(atom_counts)
    positions = jnp.arange(length_total, dtype=jnp.int32)
    return jnp.sum((positions[:, None] >= atom_ends[None, :]).astype(jnp.int32), axis=1)


def pattern_mask(pattern, row_atoms, col_atoms):
    levels = jnp.arange(pattern.shape[0], dtype=jnp.int32)
    row_onehot = (row_atoms[:, None] == levels[None, :]).astype(jnp.bfloat16)
    col_onehot = (col_atoms[:, None] == levels[None, :]).astype(jnp.bfloat16)
    per_row = jnp.dot(row_onehot, pattern.astype(jnp.bfloat16), preferred_element_type=jnp.float32)
    mask = lax.dot_general(
        per_row.astype(jnp.bfloat16), col_onehot, (((1,), (1,)), ((), ())),
        preferred_element_type=jnp.float32,
    )
    return mask > 0.5


def body(subspace, diag_block, pair_block, pair_pattern, atom_sizes, rotations):
    orb_dev = diag_block.shape[1]
    atoms_dev = pair_pattern.shape[2]
    atoms_here = lax.axis_index("atoms")
    shipped = [swapped(pair_block[r], "atoms", r) for r in range(ROUNDS)]
    shipped_pattern = [swapped(pair_pattern[r], "atoms", r) for r in range(ROUNDS)]
    own_atoms = atom_index(
        lax.dynamic_index_in_dim(atom_sizes, atoms_here, 0, keepdims=False), orb_dev
    )
    row_atom = own_atoms[:, None]
    col_atom = own_atoms[None, :]
    same_atom = 0.5 * (row_atom == col_atom).astype(jnp.float32)
    weight = (row_atom < col_atom).astype(jnp.float32) + same_atom
    weight_t = (col_atom < row_atom).astype(jnp.float32) + same_atom
    diag_sym = (
        diag_block.astype(jnp.float32) * weight + diag_block.T.astype(jnp.float32) * weight_t
    ).astype(jnp.bfloat16)
    other_pair = []
    for round_index in range(ROUNDS):
        partner = jnp.bitwise_xor(atoms_here, 1 << round_index)
        other_atoms = atom_index(
            lax.dynamic_index_in_dim(atom_sizes, partner, 0, keepdims=False), orb_dev
        )
        own_mask_t = pattern_mask(pair_pattern[round_index].T, other_atoms, own_atoms)
        own_block_t = jnp.where(own_mask_t, pair_block[round_index].T, jnp.zeros((), jnp.bfloat16))
        other_mask = pattern_mask(shipped_pattern[round_index], other_atoms, own_atoms)
        other_block = jnp.where(other_mask, shipped[round_index], jnp.zeros((), jnp.bfloat16))
        other_pair.append(
            (other_block.astype(jnp.float32) + own_block_t.astype(jnp.float32)).astype(jnp.bfloat16)
        )

    def apply_operator(values):
        result = jnp.dot(values, diag_sym, preferred_element_type=jnp.float32)
        for round_index in range(ROUNDS):
            other_rows = swapped(values, "atoms", round_index)
            result = result + jnp.dot(
                other_rows, other_pair[round_index], preferred_element_type=jnp.float32
            )
        return result

    def chebyshev(start_rows, hook):
        previous = start_rows.astype(jnp.float32)
        current = (apply_operator(start_rows) - filter_center * previous) / filter_half
        for degree_index in range(1, DEGREE):
            if degree_index == GATHER_AT:
                current = hook(current)
            if degree_index == DEGREE - 1 and gathered:
                settled, current = lax.optimization_barrier((gathered[0], current))
                gathered[0] = settled
            applied = apply_operator(current.astype(jnp.bfloat16))
            following = 2.0 * (applied - filter_center * current) / filter_half - previous
            previous, current = (current, following)
        return current

    gathered = []

    def start_rotation_gather(current):
        held, current = lax.optimization_barrier((rotations, current))
        half_rows = held.shape[1] // 2
        first_of_pair = (atoms_here % 2) == 0
        mine = jnp.where(
            first_of_pair, held[: ROTS - 1, :half_rows], held[: ROTS - 1, half_rows:]
        )
        mine = gather_pieces(mine)
        theirs = swapped(mine, "atoms", 0)
        mine_start = (atoms_here % 2) * half_rows
        whole = jnp.zeros(mine.shape[:2] + (2 * half_rows,) + mine.shape[3:], mine.dtype)
        whole = lax.dynamic_update_slice_in_dim(whole, mine, mine_start, axis=2)
        whole = lax.dynamic_update_slice_in_dim(whole, theirs, half_rows - mine_start, axis=2)
        gathered.append(whole)
        return current

    half_bands = subspace.shape[0] // 2
    first_half = chebyshev(subspace[:half_bands], start_rotation_gather)
    first_gathered = gather_bands(first_half.astype(jnp.bfloat16))
    second_half = chebyshev(subspace[half_bands:], lambda rows: rows)
    second_gathered = gather_bands(second_half.astype(jnp.bfloat16))
    rot_pieces = gathered[0]
    total_orbitals = orb_dev * lax.axis_size("atoms")
    band_count = lax.axis_size("bands")
    band_here = lax.axis_index("bands")
    all_bands = rotations.shape[1]
    basis_all = jnp.stack([first_gathered, second_gathered], axis=1).reshape(all_bands, orb_dev)
    for rotation_index in range(ROTS - 1):
        groups = []
        for group in range(band_count):
            piece = lax.dynamic_index_in_dim(
                rot_pieces, (band_here - group) % band_count, 0, keepdims=False
            )
            groups.append(
                lax.dot_general(
                    piece[rotation_index],
                    basis_all,
                    (((0,), (0,)), ((), ())),
                    preferred_element_type=jnp.float32,
                )
            )
        mixed_rows = jnp.concatenate(groups, axis=0)
        squares = atoms_sum(jnp.sum(mixed_rows * mixed_rows, axis=1))
        col_norm = jnp.sqrt(squares / total_orbitals + norm_eps)
        basis_all = (mixed_rows / col_norm[:, None]).astype(jnp.bfloat16)
    mixed_rows = lax.dot_general(
        rotations[ROTS - 1],
        basis_all,
        (((0,), (0,)), ((), ())),
        preferred_element_type=jnp.float32,
    )
    squares = atoms_sum(jnp.sum(mixed_rows * mixed_rows, axis=1))
    col_norm = jnp.sqrt(squares / total_orbitals + norm_eps)
    return mixed_rows / col_norm[:, None]


def solution(mesh):
    placed = (
        P("bands", "atoms"),
        P("atoms", None),
        P(None, "atoms", None),
        P(None, "atoms", None),
        P(),
        P(None, None, "bands"),
    )
    return jax.shard_map(
        body, mesh=mesh, in_specs=placed, out_specs=P("bands", "atoms"), check_vma=False
    )
```

```python
import jax
import jax.numpy as jnp
from jax import lax
from jax.sharding import PartitionSpec as P

ROUNDS = 2
DEGREE = 8
ROTS = 4
GATHER_AT = 2


filter_center = 0.1
filter_half = 1.25
norm_eps = 1e-06


def swapped(value, axis, stride):
    mask = 2**stride
    pairs = [(source, source ^ mask) for source in range(lax.axis_size(axis))]
    return lax.ppermute(value, axis, pairs)


def gather_bands(value):
    count = lax.axis_size("bands")
    here = lax.axis_index("bands")
    pieces = [value]
    for shift in range(1, count):
        pairs = [(source, (source + shift) % count) for source in range(count)]
        pieces.append(lax.ppermute(value, "bands", pairs))
    order = (here - jnp.arange(count, dtype=jnp.int32)) % count
    return jnp.take(jnp.stack(pieces), order, axis=0)


def gather_pieces(value):
    count = lax.axis_size("bands")
    pieces = [value]
    for shift in range(1, count):
        pairs = [(source, (source + shift) % count) for source in range(count)]
        pieces.append(lax.ppermute(value, "bands", pairs))
    return jnp.stack(pieces)


def atoms_sum(value):
    count = lax.axis_size("atoms")
    stride = 0
    while (1 << stride) < count:
        value = value + swapped(value, "atoms", stride)
        stride += 1
    return value


def atom_index(atom_counts, length_total):
    atom_ends = jnp.cumsum(atom_counts)
    positions = jnp.arange(length_total, dtype=jnp.int32)
    return jnp.sum((positions[:, None] >= atom_ends[None, :]).astype(jnp.int32), axis=1)


def pattern_mask(pattern, row_atoms, col_atoms):
    levels = jnp.arange(pattern.shape[0], dtype=jnp.int32)
    row_onehot = (row_atoms[:, None] == levels[None, :]).astype(jnp.bfloat16)
    col_onehot = (col_atoms[:, None] == levels[None, :]).astype(jnp.bfloat16)
    per_row = jnp.dot(row_onehot, pattern.astype(jnp.bfloat16), preferred_element_type=jnp.float32)
    mask = lax.dot_general(
        per_row.astype(jnp.bfloat16), col_onehot, (((1,), (1,)), ((), ())),
        preferred_element_type=jnp.float32,
    )
    return mask > 0.5


def body(subspace, diag_block, pair_block, pair_pattern, atom_sizes, rotations):
    orb_dev = diag_block.shape[1]
    atoms_dev = pair_pattern.shape[2]
    atoms_here = lax.axis_index("atoms")
    shipped = [swapped(pair_block[r], "atoms", r) for r in range(ROUNDS)]
    shipped_pattern = [swapped(pair_pattern[r], "atoms", r) for r in range(ROUNDS)]
    own_atoms = atom_index(
        lax.dynamic_index_in_dim(atom_sizes, atoms_here, 0, keepdims=False), orb_dev
    )
    row_atom = own_atoms[:, None]
    col_atom = own_atoms[None, :]
    same_atom = 0.5 * (row_atom == col_atom).astype(jnp.float32)
    weight = (row_atom < col_atom).astype(jnp.float32) + same_atom
    weight_t = (col_atom < row_atom).astype(jnp.float32) + same_atom
    diag_sym = (
        diag_block.astype(jnp.float32) * weight + diag_block.T.astype(jnp.float32) * weight_t
    ).astype(jnp.bfloat16)
    other_pair = []
    for round_index in range(ROUNDS):
        partner = jnp.bitwise_xor(atoms_here, 1 << round_index)
        other_atoms = atom_index(
            lax.dynamic_index_in_dim(atom_sizes, partner, 0, keepdims=False), orb_dev
        )
        own_mask_t = pattern_mask(pair_pattern[round_index].T, other_atoms, own_atoms)
        own_block_t = jnp.where(own_mask_t, pair_block[round_index].T, jnp.zeros((), jnp.bfloat16))
        other_mask = pattern_mask(shipped_pattern[round_index], other_atoms, own_atoms)
        other_block = jnp.where(other_mask, shipped[round_index], jnp.zeros((), jnp.bfloat16))
        other_pair.append(
            (other_block.astype(jnp.float32) + own_block_t.astype(jnp.float32)).astype(jnp.bfloat16)
        )

    def apply_operator(values):
        result = jnp.dot(values, diag_sym, preferred_element_type=jnp.float32)
        for round_index in range(ROUNDS):
            other_rows = swapped(values, "atoms", round_index)
            result = result + jnp.dot(
                other_rows, other_pair[round_index], preferred_element_type=jnp.float32
            )
        return result

    def chebyshev(start_rows, hook):
        previous = start_rows.astype(jnp.float32)
        current = (apply_operator(start_rows) - filter_center * previous) / filter_half
        for degree_index in range(1, DEGREE):
            if degree_index == GATHER_AT:
                current = hook(current)
            if degree_index == DEGREE - 1 and gathered:
                whole = gathered[0]
                count = whole.shape[0]
                block = whole.shape[2] // count
                here = lax.axis_index("bands")
                first_step = jnp.concatenate(
                    [
                        lax.dynamic_slice_in_dim(
                            whole[:, 0], ((here - shift) % count) * block, block, axis=1
                        )
                        for shift in range(count)
                    ],
                    axis=1,
                )
                settled, first_step, current = lax.optimization_barrier(
                    (whole, first_step, current)
                )
                gathered[0] = settled
                gathered.append(first_step)
            applied = apply_operator(current.astype(jnp.bfloat16))
            following = 2.0 * (applied - filter_center * current) / filter_half - previous
            previous, current = (current, following)
        return current

    gathered = []

    def start_rotation_gather(current):
        held, current = lax.optimization_barrier((rotations, current))
        half_rows = held.shape[1] // 2
        first_of_pair = (atoms_here % 2) == 0
        mine = jnp.where(
            first_of_pair, held[: ROTS - 1, :half_rows], held[: ROTS - 1, half_rows:]
        )
        mine = gather_pieces(mine)
        theirs = swapped(mine, "atoms", 0)
        mine_start = (atoms_here % 2) * half_rows
        whole = jnp.zeros(mine.shape[:2] + (2 * half_rows,) + mine.shape[3:], mine.dtype)
        whole = lax.dynamic_update_slice_in_dim(whole, mine, mine_start, axis=2)
        whole = lax.dynamic_update_slice_in_dim(whole, theirs, half_rows - mine_start, axis=2)
        gathered.append(whole)
        return current

    half_bands = subspace.shape[0] // 2
    first_half = chebyshev(subspace[:half_bands], start_rotation_gather)
    first_gathered = gather_pieces(first_half.astype(jnp.bfloat16))
    second_half = chebyshev(subspace[half_bands:], lambda rows: rows)
    second_gathered = gather_pieces(second_half.astype(jnp.bfloat16))
    rot_pieces = gathered[0]
    total_orbitals = orb_dev * lax.axis_size("atoms")
    band_count = lax.axis_size("bands")
    band_here = lax.axis_index("bands")
    all_bands = rotations.shape[1]
    basis_all = jnp.stack([first_gathered, second_gathered], axis=1).reshape(all_bands, orb_dev)
    first_step = gathered[1]
    for rotation_index in range(ROTS - 1):
        groups = []
        for group in range(band_count):
            shift = (band_here - group) % band_count
            if rotation_index == 0:
                piece = lax.dynamic_index_in_dim(first_step, shift, 0, keepdims=False)
            else:
                piece = lax.dynamic_index_in_dim(
                    rot_pieces, shift, 0, keepdims=False
                )[rotation_index]
            groups.append(
                lax.dot_general(
                    piece,
                    basis_all,
                    (((0,), (0,)), ((), ())),
                    preferred_element_type=jnp.float32,
                )
            )
        mixed_rows = jnp.concatenate(groups, axis=0)
        squares = atoms_sum(jnp.sum(mixed_rows * mixed_rows, axis=1))
        col_norm = jnp.sqrt(squares / total_orbitals + norm_eps)
        basis_all = (mixed_rows / col_norm[:, None]).astype(jnp.bfloat16)
    mixed_rows = lax.dot_general(
        rotations[ROTS - 1],
        basis_all,
        (((0,), (0,)), ((), ())),
        preferred_element_type=jnp.float32,
    )
    squares = atoms_sum(jnp.sum(mixed_rows * mixed_rows, axis=1))
    col_norm = jnp.sqrt(squares / total_orbitals + norm_eps)
    return mixed_rows / col_norm[:, None]


def solution(mesh):
    placed = (
        P("bands", "atoms"),
        P("atoms", None),
        P(None, "atoms", None),
        P(None, "atoms", None),
        P(),
        P(None, None, "bands"),
    )
    return jax.shard_map(
        body, mesh=mesh, in_specs=placed, out_specs=P("bands", "atoms"), check_vma=False
    )
```

```python
import jax
import jax.numpy as jnp
from jax import lax
from jax.sharding import PartitionSpec as P

ROUNDS = 2
DEGREE = 8
ROTS = 4
GATHER_AT = 1


filter_center = 0.1
filter_half = 1.25
norm_eps = 1e-06


def swapped(value, axis, stride):
    mask = 2**stride
    pairs = [(source, source ^ mask) for source in range(lax.axis_size(axis))]
    return lax.ppermute(value, axis, pairs)


def gather_bands(value):
    count = lax.axis_size("bands")
    here = lax.axis_index("bands")
    pieces = [value]
    for shift in range(1, count):
        pairs = [(source, (source + shift) % count) for source in range(count)]
        pieces.append(lax.ppermute(value, "bands", pairs))
    order = (here - jnp.arange(count, dtype=jnp.int32)) % count
    return jnp.take(jnp.stack(pieces), order, axis=0)


def gather_pieces(value):
    count = lax.axis_size("bands")
    pieces = [value]
    for shift in range(1, count):
        pairs = [(source, (source + shift) % count) for source in range(count)]
        pieces.append(lax.ppermute(value, "bands", pairs))
    return jnp.stack(pieces)


def atoms_sum(value):
    count = lax.axis_size("atoms")
    stride = 0
    while (1 << stride) < count:
        value = value + swapped(value, "atoms", stride)
        stride += 1
    return value


def atom_index(atom_counts, length_total):
    atom_ends = jnp.cumsum(atom_counts)
    positions = jnp.arange(length_total, dtype=jnp.int32)
    return jnp.sum((positions[:, None] >= atom_ends[None, :]).astype(jnp.int32), axis=1)


def pattern_mask(pattern, row_atoms, col_atoms):
    levels = jnp.arange(pattern.shape[0], dtype=jnp.int32)
    row_onehot = (row_atoms[:, None] == levels[None, :]).astype(jnp.bfloat16)
    col_onehot = (col_atoms[:, None] == levels[None, :]).astype(jnp.bfloat16)
    per_row = jnp.dot(row_onehot, pattern.astype(jnp.bfloat16), preferred_element_type=jnp.float32)
    mask = lax.dot_general(
        per_row.astype(jnp.bfloat16), col_onehot, (((1,), (1,)), ((), ())),
        preferred_element_type=jnp.float32,
    )
    return mask > 0.5


def body(subspace, diag_block, pair_block, pair_pattern, atom_sizes, rotations):
    orb_dev = diag_block.shape[1]
    atoms_dev = pair_pattern.shape[2]
    atoms_here = lax.axis_index("atoms")
    shipped = [swapped(pair_block[r], "atoms", r) for r in range(ROUNDS)]
    shipped_pattern = [swapped(pair_pattern[r], "atoms", r) for r in range(ROUNDS)]
    own_atoms = atom_index(
        lax.dynamic_index_in_dim(atom_sizes, atoms_here, 0, keepdims=False), orb_dev
    )
    row_atom = own_atoms[:, None]
    col_atom = own_atoms[None, :]
    same_atom = 0.5 * (row_atom == col_atom).astype(jnp.float32)
    weight = (row_atom < col_atom).astype(jnp.float32) + same_atom
    weight_t = (col_atom < row_atom).astype(jnp.float32) + same_atom
    diag_sym = (
        diag_block.astype(jnp.float32) * weight + diag_block.T.astype(jnp.float32) * weight_t
    ).astype(jnp.bfloat16)
    other_pair = []
    for round_index in range(ROUNDS):
        partner = jnp.bitwise_xor(atoms_here, 1 << round_index)
        other_atoms = atom_index(
            lax.dynamic_index_in_dim(atom_sizes, partner, 0, keepdims=False), orb_dev
        )
        own_mask_t = pattern_mask(pair_pattern[round_index].T, other_atoms, own_atoms)
        own_block_t = jnp.where(own_mask_t, pair_block[round_index].T, jnp.zeros((), jnp.bfloat16))
        other_mask = pattern_mask(shipped_pattern[round_index], other_atoms, own_atoms)
        other_block = jnp.where(other_mask, shipped[round_index], jnp.zeros((), jnp.bfloat16))
        other_pair.append(
            (other_block.astype(jnp.float32) + own_block_t.astype(jnp.float32)).astype(jnp.bfloat16)
        )

    def apply_operator(values):
        result = jnp.dot(values, diag_sym, preferred_element_type=jnp.float32)
        for round_index in range(ROUNDS):
            other_rows = swapped(values, "atoms", round_index)
            result = result + jnp.dot(
                other_rows, other_pair[round_index], preferred_element_type=jnp.float32
            )
        return result

    def chebyshev(start_rows, hook):
        previous = start_rows.astype(jnp.float32)
        current = (apply_operator(start_rows) - filter_center * previous) / filter_half
        for degree_index in range(1, DEGREE):
            if degree_index == GATHER_AT:
                current = hook(current)
            if degree_index == DEGREE - 1 and gathered:
                settled, current = lax.optimization_barrier((gathered[0], current))
                gathered[0] = settled
            applied = apply_operator(current.astype(jnp.bfloat16))
            following = 2.0 * (applied - filter_center * current) / filter_half - previous
            previous, current = (current, following)
        return current

    gathered = []

    def start_rotation_gather(current):
        held, current = lax.optimization_barrier((rotations, current))
        half_rows = held.shape[1] // 2
        first_of_pair = (atoms_here % 2) == 0
        mine = jnp.where(
            first_of_pair, held[: ROTS - 1, :half_rows], held[: ROTS - 1, half_rows:]
        )
        mine = gather_pieces(mine)
        theirs = swapped(mine, "atoms", 0)
        mine_start = (atoms_here % 2) * half_rows
        whole = jnp.zeros(mine.shape[:2] + (2 * half_rows,) + mine.shape[3:], mine.dtype)
        whole = lax.dynamic_update_slice_in_dim(whole, mine, mine_start, axis=2)
        whole = lax.dynamic_update_slice_in_dim(whole, theirs, half_rows - mine_start, axis=2)
        gathered.append(whole)
        return current

    half_bands = subspace.shape[0] // 2
    first_half = chebyshev(subspace[:half_bands], start_rotation_gather)
    first_gathered = gather_bands(first_half.astype(jnp.bfloat16))
    second_half = chebyshev(subspace[half_bands:], lambda rows: rows)
    second_gathered = gather_bands(second_half.astype(jnp.bfloat16))
    rot_pieces = gathered[0]
    total_orbitals = orb_dev * lax.axis_size("atoms")
    band_count = lax.axis_size("bands")
    band_here = lax.axis_index("bands")
    all_bands = rotations.shape[1]
    basis_all = jnp.stack([first_gathered, second_gathered], axis=1).reshape(all_bands, orb_dev)
    for rotation_index in range(ROTS - 1):
        groups = []
        for group in range(band_count):
            piece = lax.dynamic_index_in_dim(
                rot_pieces, (band_here - group) % band_count, 0, keepdims=False
            )
            groups.append(
                lax.dot_general(
                    piece[rotation_index],
                    basis_all,
                    (((0,), (0,)), ((), ())),
                    preferred_element_type=jnp.float32,
                )
            )
        mixed_rows = jnp.concatenate(groups, axis=0)
        squares = atoms_sum(jnp.sum(mixed_rows * mixed_rows, axis=1))
        col_norm = jnp.sqrt(squares / total_orbitals + norm_eps)
        basis_all = (mixed_rows / col_norm[:, None]).astype(jnp.bfloat16)
    mixed_rows = lax.dot_general(
        rotations[ROTS - 1],
        basis_all,
        (((0,), (0,)), ((), ())),
        preferred_element_type=jnp.float32,
    )
    squares = atoms_sum(jnp.sum(mixed_rows * mixed_rows, axis=1))
    col_norm = jnp.sqrt(squares / total_orbitals + norm_eps)
    return mixed_rows / col_norm[:, None]


def solution(mesh):
    placed = (
        P("bands", "atoms"),
        P("atoms", None),
        P(None, "atoms", None),
        P(None, "atoms", None),
        P(),
        P(None, None, "bands"),
    )
    return jax.shard_map(
        body, mesh=mesh, in_specs=placed, out_specs=P("bands", "atoms"), check_vma=False
    )
```

```python
import jax
import jax.numpy as jnp
from jax import lax
from jax.sharding import PartitionSpec as P

ROUNDS = 2
DEGREE = 8
ROTS = 4
GATHER_AT = 3


filter_center = 0.1
filter_half = 1.25
norm_eps = 1e-06


def swapped(value, axis, stride):
    mask = 2**stride
    pairs = [(source, source ^ mask) for source in range(lax.axis_size(axis))]
    return lax.ppermute(value, axis, pairs)


def gather_bands(value):
    count = lax.axis_size("bands")
    here = lax.axis_index("bands")
    pieces = [value]
    for shift in range(1, count):
        pairs = [(source, (source + shift) % count) for source in range(count)]
        pieces.append(lax.ppermute(value, "bands", pairs))
    order = (here - jnp.arange(count, dtype=jnp.int32)) % count
    return jnp.take(jnp.stack(pieces), order, axis=0)


def gather_pieces(value):
    count = lax.axis_size("bands")
    pieces = [value]
    for shift in range(1, count):
        pairs = [(source, (source + shift) % count) for source in range(count)]
        pieces.append(lax.ppermute(value, "bands", pairs))
    return jnp.stack(pieces)


def atoms_sum(value):
    count = lax.axis_size("atoms")
    stride = 0
    while (1 << stride) < count:
        value = value + swapped(value, "atoms", stride)
        stride += 1
    return value


def atom_index(atom_counts, length_total):
    atom_ends = jnp.cumsum(atom_counts)
    positions = jnp.arange(length_total, dtype=jnp.int32)
    return jnp.sum((positions[:, None] >= atom_ends[None, :]).astype(jnp.int32), axis=1)


def pattern_mask(pattern, row_atoms, col_atoms):
    levels = jnp.arange(pattern.shape[0], dtype=jnp.int32)
    row_onehot = (row_atoms[:, None] == levels[None, :]).astype(jnp.bfloat16)
    col_onehot = (col_atoms[:, None] == levels[None, :]).astype(jnp.bfloat16)
    per_row = jnp.dot(row_onehot, pattern.astype(jnp.bfloat16), preferred_element_type=jnp.float32)
    mask = lax.dot_general(
        per_row.astype(jnp.bfloat16), col_onehot, (((1,), (1,)), ((), ())),
        preferred_element_type=jnp.float32,
    )
    return mask > 0.5


def body(subspace, diag_block, pair_block, pair_pattern, atom_sizes, rotations):
    orb_dev = diag_block.shape[1]
    atoms_dev = pair_pattern.shape[2]
    atoms_here = lax.axis_index("atoms")
    shipped = [swapped(pair_block[r], "atoms", r) for r in range(ROUNDS)]
    shipped_pattern = [swapped(pair_pattern[r], "atoms", r) for r in range(ROUNDS)]
    own_atoms = atom_index(
        lax.dynamic_index_in_dim(atom_sizes, atoms_here, 0, keepdims=False), orb_dev
    )
    row_atom = own_atoms[:, None]
    col_atom = own_atoms[None, :]
    same_atom = 0.5 * (row_atom == col_atom).astype(jnp.float32)
    weight = (row_atom < col_atom).astype(jnp.float32) + same_atom
    weight_t = (col_atom < row_atom).astype(jnp.float32) + same_atom
    diag_sym = (
        diag_block.astype(jnp.float32) * weight + diag_block.T.astype(jnp.float32) * weight_t
    ).astype(jnp.bfloat16)
    other_pair = []
    for round_index in range(ROUNDS):
        partner = jnp.bitwise_xor(atoms_here, 1 << round_index)
        other_atoms = atom_index(
            lax.dynamic_index_in_dim(atom_sizes, partner, 0, keepdims=False), orb_dev
        )
        own_mask_t = pattern_mask(pair_pattern[round_index].T, other_atoms, own_atoms)
        own_block_t = jnp.where(own_mask_t, pair_block[round_index].T, jnp.zeros((), jnp.bfloat16))
        other_mask = pattern_mask(shipped_pattern[round_index], other_atoms, own_atoms)
        other_block = jnp.where(other_mask, shipped[round_index], jnp.zeros((), jnp.bfloat16))
        other_pair.append(
            (other_block.astype(jnp.float32) + own_block_t.astype(jnp.float32)).astype(jnp.bfloat16)
        )

    def apply_operator(values):
        result = jnp.dot(values, diag_sym, preferred_element_type=jnp.float32)
        for round_index in range(ROUNDS):
            other_rows = swapped(values, "atoms", round_index)
            result = result + jnp.dot(
                other_rows, other_pair[round_index], preferred_element_type=jnp.float32
            )
        return result

    def chebyshev(start_rows, hook):
        previous = start_rows.astype(jnp.float32)
        current = (apply_operator(start_rows) - filter_center * previous) / filter_half
        for degree_index in range(1, DEGREE):
            if degree_index == GATHER_AT:
                current = hook(current)
            if degree_index == DEGREE - 1 and gathered:
                settled, current = lax.optimization_barrier((gathered[0], current))
                gathered[0] = settled
            applied = apply_operator(current.astype(jnp.bfloat16))
            following = 2.0 * (applied - filter_center * current) / filter_half - previous
            previous, current = (current, following)
        return current

    gathered = []

    def start_rotation_gather(current):
        held, current = lax.optimization_barrier((rotations, current))
        half_rows = held.shape[1] // 2
        first_of_pair = (atoms_here % 2) == 0
        mine = jnp.where(
            first_of_pair, held[: ROTS - 1, :half_rows], held[: ROTS - 1, half_rows:]
        )
        mine = gather_pieces(mine)
        theirs = swapped(mine, "atoms", 0)
        mine_start = (atoms_here % 2) * half_rows
        whole = jnp.zeros(mine.shape[:2] + (2 * half_rows,) + mine.shape[3:], mine.dtype)
        whole = lax.dynamic_update_slice_in_dim(whole, mine, mine_start, axis=2)
        whole = lax.dynamic_update_slice_in_dim(whole, theirs, half_rows - mine_start, axis=2)
        gathered.append(whole)
        return current

    half_bands = subspace.shape[0] // 2
    first_half = chebyshev(subspace[:half_bands], start_rotation_gather)
    first_gathered = gather_bands(first_half.astype(jnp.bfloat16))
    second_half = chebyshev(subspace[half_bands:], lambda rows: rows)
    second_gathered = gather_bands(second_half.astype(jnp.bfloat16))
    rot_pieces = gathered[0]
    total_orbitals = orb_dev * lax.axis_size("atoms")
    band_count = lax.axis_size("bands")
    band_here = lax.axis_index("bands")
    all_bands = rotations.shape[1]
    basis_all = jnp.stack([first_gathered, second_gathered], axis=1).reshape(all_bands, orb_dev)
    for rotation_index in range(ROTS - 1):
        groups = []
        for group in range(band_count):
            piece = lax.dynamic_index_in_dim(
                rot_pieces, (band_here - group) % band_count, 0, keepdims=False
            )
            groups.append(
                lax.dot_general(
                    piece[rotation_index],
                    basis_all,
                    (((0,), (0,)), ((), ())),
                    preferred_element_type=jnp.float32,
                )
            )
        mixed_rows = jnp.concatenate(groups, axis=0)
        squares = atoms_sum(jnp.sum(mixed_rows * mixed_rows, axis=1))
        col_norm = jnp.sqrt(squares / total_orbitals + norm_eps)
        basis_all = (mixed_rows / col_norm[:, None]).astype(jnp.bfloat16)
    mixed_rows = lax.dot_general(
        rotations[ROTS - 1],
        basis_all,
        (((0,), (0,)), ((), ())),
        preferred_element_type=jnp.float32,
    )
    squares = atoms_sum(jnp.sum(mixed_rows * mixed_rows, axis=1))
    col_norm = jnp.sqrt(squares / total_orbitals + norm_eps)
    return mixed_rows / col_norm[:, None]


def solution(mesh):
    placed = (
        P("bands", "atoms"),
        P("atoms", None),
        P(None, "atoms", None),
        P(None, "atoms", None),
        P(),
        P(None, None, "bands"),
    )
    return jax.shard_map(
        body, mesh=mesh, in_specs=placed, out_specs=P("bands", "atoms"), check_vma=False
    )
```

```python
import jax
import jax.numpy as jnp
from jax import lax
from jax.sharding import PartitionSpec as P

ROUNDS = 2
DEGREE = 8
ROTS = 4
GATHER_AT = 2


filter_center = 0.1
filter_half = 1.25
norm_eps = 1e-06


def swapped(value, axis, stride):
    mask = 2**stride
    pairs = [(source, source ^ mask) for source in range(lax.axis_size(axis))]
    return lax.ppermute(value, axis, pairs)


def gather_bands(value):
    count = lax.axis_size("bands")
    here = lax.axis_index("bands")
    pieces = [value]
    for shift in range(1, count):
        pairs = [(source, (source + shift) % count) for source in range(count)]
        pieces.append(lax.ppermute(value, "bands", pairs))
    order = (here - jnp.arange(count, dtype=jnp.int32)) % count
    return jnp.take(jnp.stack(pieces), order, axis=0)


def gather_pieces(value):
    count = lax.axis_size("bands")
    pieces = [value]
    for shift in range(1, count):
        pairs = [(source, (source + shift) % count) for source in range(count)]
        pieces.append(lax.ppermute(value, "bands", pairs))
    return jnp.stack(pieces)


def atoms_sum(value):
    count = lax.axis_size("atoms")
    stride = 0
    while (1 << stride) < count:
        value = value + swapped(value, "atoms", stride)
        stride += 1
    return value


def atom_index(atom_counts, length_total):
    atom_ends = jnp.cumsum(atom_counts)
    positions = jnp.arange(length_total, dtype=jnp.int32)
    return jnp.sum((positions[:, None] >= atom_ends[None, :]).astype(jnp.int32), axis=1)


def pattern_mask(pattern, row_atoms, col_atoms):
    levels = jnp.arange(pattern.shape[0], dtype=jnp.int32)
    row_onehot = (row_atoms[:, None] == levels[None, :]).astype(jnp.bfloat16)
    col_onehot = (col_atoms[:, None] == levels[None, :]).astype(jnp.bfloat16)
    per_row = jnp.dot(row_onehot, pattern.astype(jnp.bfloat16), preferred_element_type=jnp.float32)
    mask = lax.dot_general(
        per_row.astype(jnp.bfloat16), col_onehot, (((1,), (1,)), ((), ())),
        preferred_element_type=jnp.float32,
    )
    return mask > 0.5


def body(subspace, diag_block, pair_block, pair_pattern, atom_sizes, rotations):
    orb_dev = diag_block.shape[1]
    atoms_dev = pair_pattern.shape[2]
    atoms_here = lax.axis_index("atoms")
    shipped = [swapped(pair_block[r], "atoms", r) for r in range(ROUNDS)]
    shipped_pattern = [swapped(pair_pattern[r], "atoms", r) for r in range(ROUNDS)]
    own_atoms = atom_index(
        lax.dynamic_index_in_dim(atom_sizes, atoms_here, 0, keepdims=False), orb_dev
    )
    row_atom = own_atoms[:, None]
    col_atom = own_atoms[None, :]
    same_atom = 0.5 * (row_atom == col_atom).astype(jnp.float32)
    weight = (row_atom < col_atom).astype(jnp.float32) + same_atom
    weight_t = (col_atom < row_atom).astype(jnp.float32) + same_atom
    diag_sym = (
        diag_block.astype(jnp.float32) * weight + diag_block.T.astype(jnp.float32) * weight_t
    ).astype(jnp.bfloat16)
    other_pair = []
    for round_index in range(ROUNDS):
        partner = jnp.bitwise_xor(atoms_here, 1 << round_index)
        other_atoms = atom_index(
            lax.dynamic_index_in_dim(atom_sizes, partner, 0, keepdims=False), orb_dev
        )
        own_mask_t = pattern_mask(pair_pattern[round_index].T, other_atoms, own_atoms)
        own_block_t = jnp.where(own_mask_t, pair_block[round_index].T, jnp.zeros((), jnp.bfloat16))
        other_mask = pattern_mask(shipped_pattern[round_index], other_atoms, own_atoms)
        other_block = jnp.where(other_mask, shipped[round_index], jnp.zeros((), jnp.bfloat16))
        other_pair.append(
            (other_block.astype(jnp.float32) + own_block_t.astype(jnp.float32)).astype(jnp.bfloat16)
        )

    def apply_operator(values):
        result = jnp.dot(values, diag_sym, preferred_element_type=jnp.float32)
        for round_index in range(ROUNDS):
            other_rows = swapped(values, "atoms", round_index)
            result = result + jnp.dot(
                other_rows, other_pair[round_index], preferred_element_type=jnp.float32
            )
        return result

    def chebyshev(start_rows, hook):
        previous = start_rows.astype(jnp.float32)
        current = (apply_operator(start_rows) - filter_center * previous) / filter_half
        for degree_index in range(1, DEGREE):
            if degree_index == GATHER_AT:
                current = hook(current)
            if degree_index == DEGREE - 1 and gathered:
                settled, current = lax.optimization_barrier((gathered[0], current))
                gathered[0] = settled
            applied = apply_operator(current.astype(jnp.bfloat16))
            following = 2.0 * (applied - filter_center * current) / filter_half - previous
            previous, current = (current, following)
        return current

    gathered = []

    def start_rotation_gather(current):
        held, current = lax.optimization_barrier((rotations, current))
        half_rows = held.shape[1] // 2
        first_of_pair = (atoms_here % 2) == 0
        mine = jnp.where(
            first_of_pair, held[:, :half_rows], held[:, half_rows:]
        )
        mine = gather_pieces(mine)
        theirs = swapped(mine, "atoms", 0)
        mine_start = (atoms_here % 2) * half_rows
        whole = jnp.zeros(mine.shape[:2] + (2 * half_rows,) + mine.shape[3:], mine.dtype)
        whole = lax.dynamic_update_slice_in_dim(whole, mine, mine_start, axis=2)
        whole = lax.dynamic_update_slice_in_dim(whole, theirs, half_rows - mine_start, axis=2)
        gathered.append(whole)
        return current

    half_bands = subspace.shape[0] // 2
    first_half = chebyshev(subspace[:half_bands], start_rotation_gather)
    first_gathered = gather_bands(first_half.astype(jnp.bfloat16))
    second_half = chebyshev(subspace[half_bands:], lambda rows: rows)
    second_gathered = gather_bands(second_half.astype(jnp.bfloat16))
    rot_pieces = gathered[0]
    total_orbitals = orb_dev * lax.axis_size("atoms")
    band_count = lax.axis_size("bands")
    band_here = lax.axis_index("bands")
    all_bands = rotations.shape[1]
    basis_all = jnp.stack([first_gathered, second_gathered], axis=1).reshape(all_bands, orb_dev)
    for rotation_index in range(ROTS - 1):
        groups = []
        for group in range(band_count):
            piece = lax.dynamic_index_in_dim(
                rot_pieces, (band_here - group) % band_count, 0, keepdims=False
            )
            groups.append(
                lax.dot_general(
                    piece[rotation_index],
                    basis_all,
                    (((0,), (0,)), ((), ())),
                    preferred_element_type=jnp.float32,
                )
            )
        mixed_rows = jnp.concatenate(groups, axis=0)
        squares = atoms_sum(jnp.sum(mixed_rows * mixed_rows, axis=1))
        col_norm = jnp.sqrt(squares / total_orbitals + norm_eps)
        basis_all = (mixed_rows / col_norm[:, None]).astype(jnp.bfloat16)
    mixed_rows = lax.dot_general(
        rot_pieces[0, ROTS - 1],
        basis_all,
        (((0,), (0,)), ((), ())),
        preferred_element_type=jnp.float32,
    )
    squares = atoms_sum(jnp.sum(mixed_rows * mixed_rows, axis=1))
    col_norm = jnp.sqrt(squares / total_orbitals + norm_eps)
    return mixed_rows / col_norm[:, None]


def solution(mesh):
    placed = (
        P("bands", "atoms"),
        P("atoms", None),
        P(None, "atoms", None),
        P(None, "atoms", None),
        P(),
        P(None, None, "bands"),
    )
    return jax.shard_map(
        body, mesh=mesh, in_specs=placed, out_specs=P("bands", "atoms"), check_vma=False
    )
```

```python
import jax
import jax.numpy as jnp
from jax import lax
from jax.sharding import PartitionSpec as P

ROUNDS = 2
DEGREE = 8
ROTS = 4
GATHER_AT = 2


filter_center = 0.1
filter_half = 1.25
norm_eps = 1e-06


def swapped(value, axis, stride):
    mask = 2**stride
    pairs = [(source, source ^ mask) for source in range(lax.axis_size(axis))]
    return lax.ppermute(value, axis, pairs)


def gather_bands(value):
    count = lax.axis_size("bands")
    here = lax.axis_index("bands")
    pieces = [value]
    for shift in range(1, count):
        pairs = [(source, (source + shift) % count) for source in range(count)]
        pieces.append(lax.ppermute(value, "bands", pairs))
    order = (here - jnp.arange(count, dtype=jnp.int32)) % count
    return jnp.take(jnp.stack(pieces), order, axis=0)


def gather_pieces(value):
    count = lax.axis_size("bands")
    pieces = [value]
    for shift in range(1, count):
        pairs = [(source, (source + shift) % count) for source in range(count)]
        pieces.append(lax.ppermute(value, "bands", pairs))
    return jnp.stack(pieces)


def atoms_sum(value):
    count = lax.axis_size("atoms")
    stride = 0
    while (1 << stride) < count:
        value = value + swapped(value, "atoms", stride)
        stride += 1
    return value


def atom_index(atom_counts, length_total):
    atom_ends = jnp.cumsum(atom_counts)
    positions = jnp.arange(length_total, dtype=jnp.int32)
    return jnp.sum((positions[:, None] >= atom_ends[None, :]).astype(jnp.int32), axis=1)


def pattern_mask(pattern, row_atoms, col_atoms):
    levels = jnp.arange(pattern.shape[0], dtype=jnp.int32)
    row_onehot = (row_atoms[:, None] == levels[None, :]).astype(jnp.bfloat16)
    col_onehot = (col_atoms[:, None] == levels[None, :]).astype(jnp.bfloat16)
    per_row = jnp.dot(row_onehot, pattern.astype(jnp.bfloat16), preferred_element_type=jnp.float32)
    mask = lax.dot_general(
        per_row.astype(jnp.bfloat16), col_onehot, (((1,), (1,)), ((), ())),
        preferred_element_type=jnp.float32,
    )
    return mask > 0.5


def body(subspace, diag_block, pair_block, pair_pattern, atom_sizes, rotations):
    orb_dev = diag_block.shape[1]
    atoms_dev = pair_pattern.shape[2]
    atoms_here = lax.axis_index("atoms")
    shipped = [swapped(pair_block[r], "atoms", r) for r in range(ROUNDS)]
    shipped_pattern = [swapped(pair_pattern[r], "atoms", r) for r in range(ROUNDS)]
    own_atoms = atom_index(
        lax.dynamic_index_in_dim(atom_sizes, atoms_here, 0, keepdims=False), orb_dev
    )
    row_atom = own_atoms[:, None]
    col_atom = own_atoms[None, :]
    same_atom = 0.5 * (row_atom == col_atom).astype(jnp.float32)
    weight = (row_atom < col_atom).astype(jnp.float32) + same_atom
    weight_t = (col_atom < row_atom).astype(jnp.float32) + same_atom
    diag_sym = (
        diag_block.astype(jnp.float32) * weight + diag_block.T.astype(jnp.float32) * weight_t
    ).astype(jnp.bfloat16)
    other_pair = []
    for round_index in range(ROUNDS):
        partner = jnp.bitwise_xor(atoms_here, 1 << round_index)
        other_atoms = atom_index(
            lax.dynamic_index_in_dim(atom_sizes, partner, 0, keepdims=False), orb_dev
        )
        own_mask_t = pattern_mask(pair_pattern[round_index].T, other_atoms, own_atoms)
        own_block_t = jnp.where(own_mask_t, pair_block[round_index].T, jnp.zeros((), jnp.bfloat16))
        other_mask = pattern_mask(shipped_pattern[round_index], other_atoms, own_atoms)
        other_block = jnp.where(other_mask, shipped[round_index], jnp.zeros((), jnp.bfloat16))
        other_pair.append(
            (other_block.astype(jnp.float32) + own_block_t.astype(jnp.float32)).astype(jnp.bfloat16)
        )

    def apply_operator(values):
        result = jnp.dot(values, diag_sym, preferred_element_type=jnp.float32)
        for round_index in range(ROUNDS):
            other_rows = swapped(values, "atoms", round_index)
            result = result + jnp.dot(
                other_rows, other_pair[round_index], preferred_element_type=jnp.float32
            )
        return result

    def chebyshev(start_rows, hook):
        previous = start_rows.astype(jnp.float32)
        current = (apply_operator(start_rows) - filter_center * previous) / filter_half
        for degree_index in range(1, DEGREE):
            if degree_index == GATHER_AT:
                current = hook(current)
            if degree_index == DEGREE - 1 and gathered:
                settled, last_cols, current = lax.optimization_barrier(
                    (gathered[0], rotations[ROTS - 1], current)
                )
                gathered[0] = settled
                gathered.append(last_cols)
            applied = apply_operator(current.astype(jnp.bfloat16))
            following = 2.0 * (applied - filter_center * current) / filter_half - previous
            previous, current = (current, following)
        return current

    gathered = []

    def start_rotation_gather(current):
        held, current = lax.optimization_barrier((rotations, current))
        half_rows = held.shape[1] // 2
        first_of_pair = (atoms_here % 2) == 0
        mine = jnp.where(
            first_of_pair, held[: ROTS - 1, :half_rows], held[: ROTS - 1, half_rows:]
        )
        mine = gather_pieces(mine)
        theirs = swapped(mine, "atoms", 0)
        mine_start = (atoms_here % 2) * half_rows
        whole = jnp.zeros(mine.shape[:2] + (2 * half_rows,) + mine.shape[3:], mine.dtype)
        whole = lax.dynamic_update_slice_in_dim(whole, mine, mine_start, axis=2)
        whole = lax.dynamic_update_slice_in_dim(whole, theirs, half_rows - mine_start, axis=2)
        gathered.append(whole)
        return current

    half_bands = subspace.shape[0] // 2
    first_half = chebyshev(subspace[:half_bands], start_rotation_gather)
    first_gathered = gather_bands(first_half.astype(jnp.bfloat16))
    second_half = chebyshev(subspace[half_bands:], lambda rows: rows)
    second_gathered = gather_bands(second_half.astype(jnp.bfloat16))
    rot_pieces = gathered[0]
    total_orbitals = orb_dev * lax.axis_size("atoms")
    band_count = lax.axis_size("bands")
    band_here = lax.axis_index("bands")
    all_bands = rotations.shape[1]
    basis_all = jnp.stack([first_gathered, second_gathered], axis=1).reshape(all_bands, orb_dev)
    for rotation_index in range(ROTS - 1):
        groups = []
        for group in range(band_count):
            piece = lax.dynamic_index_in_dim(
                rot_pieces, (band_here - group) % band_count, 0, keepdims=False
            )
            groups.append(
                lax.dot_general(
                    piece[rotation_index],
                    basis_all,
                    (((0,), (0,)), ((), ())),
                    preferred_element_type=jnp.float32,
                )
            )
        mixed_rows = jnp.concatenate(groups, axis=0)
        squares = atoms_sum(jnp.sum(mixed_rows * mixed_rows, axis=1))
        col_norm = jnp.sqrt(squares / total_orbitals + norm_eps)
        basis_all = (mixed_rows / col_norm[:, None]).astype(jnp.bfloat16)
    mixed_rows = lax.dot_general(
        gathered[1],
        basis_all,
        (((0,), (0,)), ((), ())),
        preferred_element_type=jnp.float32,
    )
    squares = atoms_sum(jnp.sum(mixed_rows * mixed_rows, axis=1))
    col_norm = jnp.sqrt(squares / total_orbitals + norm_eps)
    return mixed_rows / col_norm[:, None]


def solution(mesh):
    placed = (
        P("bands", "atoms"),
        P("atoms", None),
        P(None, "atoms", None),
        P(None, "atoms", None),
        P(),
        P(None, None, "bands"),
    )
    return jax.shard_map(
        body, mesh=mesh, in_specs=placed, out_specs=P("bands", "atoms"), check_vma=False
    )
```
